256 devices in a mesh: seq: 32 (over x_hi, z, core), tp: 8 (over y, x_lo).
Axes of the slice: x: 4 (x_hi: 2, x_lo: 2; x = x_hi * 2 + x_lo), y: 4, z: 8, core: 2. Of those that a mesh axis runs over, the one named last changes fastest.
Arguments:
- proj: bfloat16 [4096, 3, 8192], P('seq', None, 'tp'), may hold values from -6 to 6
- cotangent: bfloat16 [4096, 8192], P('seq', 'tp'), may hold values from -6 to 6
- out_weight: bfloat16 [8192, 8192], P('seq', 'tp'), may hold values from -0.125 to 0.125
- short_weight: float32 [7, 3, 8192], P(None, None, 'tp'), may hold values from -2 to 2
- long_filter: float32 [4096, 8192], P('seq', 'tp')
Outputs:
- grad_proj: bfloat16 [4096, 3, 8192], P('seq', None, 'tp')
- grad_short: float32 [7, 3, 8192], P(None, None, 'tp')
- grad_filter: float32 [4096, 8192], P('seq', 'tp')
The draws below stay inside these ranges and needn't reach their ends.
All inputs are finite; a program needn't handle non-finite values.
Results may differ from the reference program's by a relative error of at most 0.025.
Values may be sent and summed in bfloat16 or wider, within the bound.
No kernel may reach another device: no remote copies, remote signals or barrier semaphores. Data moves between devices by JAX's collectives and lax.ppermute only.
A program may use at most 128 MiB of HBM per device.

```python
import math
import jax
import jax.numpy as jnp
from jax import lax

MODEL_DIMENSION = 8192
TAPS = 7
SEQUENCE_LENGTH = 4096
N_TP = 8


def draw_long_filter(key, part):
    random_subkeys = jax.random.split(key, 4)
    token_positions = jnp.arange(SEQUENCE_LENGTH, dtype=jnp.float32)[:, None]
    log_rate = jax.random.uniform(random_subkeys[0], (1, MODEL_DIMENSION), jnp.float32, math.log(0.05 / SEQUENCE_LENGTH), math.log(1.0 / 30.0))
    base_part = jax.random.truncated_normal(random_subkeys[1], -4.0, 4.0, (SEQUENCE_LENGTH, MODEL_DIMENSION), jnp.float32)
    decay_rate = jnp.exp(log_rate)
    decay_profile = jnp.exp(-decay_rate * token_positions) * jnp.sqrt(jnp.expm1(-2.0 * decay_rate) / jnp.expm1(-2.0 * decay_rate * SEQUENCE_LENGTH))
    spike_position = jax.random.randint(random_subkeys[2], (4,), 1, SEQUENCE_LENGTH)
    spike_falloff = jax.random.uniform(random_subkeys[3], (4, MODEL_DIMENSION), jnp.float32, 0.2, 0.5)
    for spike_index in range(4):
        elapsed_steps = (token_positions >= spike_position[spike_index].astype(jnp.float32)).astype(jnp.float32)
        decay_profile = decay_profile * (1.0 - spike_falloff[spike_index][None, :] * elapsed_steps)
    return (base_part * decay_profile).astype(jnp.float32)


def raised(values, key, source, target, parts, factor):
    def block_of(axis_at):
        return (jnp.arange(values.shape[axis_at]) // (values.shape[axis_at] // parts)).reshape((-1,) + (1,) * (values.ndim - 1 - axis_at))

    first = jax.random.permutation(key, parts)[block_of(target)]
    second = (block_of(target) + parts // 2) % parts
    return jnp.where((block_of(source) == first) | (block_of(source) == second), factor * values, values)


def levels(rng, dims, shards, low, top_value):
    factor_of = 1.0
    for position, parts in shards:
        steps = jax.random.uniform(jax.random.fold_in(jax.random.fold_in(rng, 6), position), (parts,), jnp.float32, low / len(shards), top_value / len(shards))
        factor_of = factor_of * jnp.repeat(jnp.exp(steps), dims[position] // parts).reshape((-1,) + (1,) * (len(dims) - 1 - position))
    return factor_of


def normal_values(stream_key, dims, deviation, limit, cuts=(), kind=jnp.bfloat16):
    drawn = jax.random.normal(stream_key, dims, jnp.float32) * deviation
    if len(cuts) > 0:
        drawn = levels(stream_key, dims, cuts, -0.22, 0.18) * drawn
    return jnp.clip(drawn, min=-limit, max=limit).astype(kind)


def gaussian_with(own_key, shape, spread, most, cuts, heavy, kind=jnp.bfloat16):
    entries = spread * jax.random.normal(own_key, shape, jnp.float32)
    if cuts:
        entries = entries * levels(own_key, shape, cuts, -0.22, 0.18)
    return jnp.clip(raised(entries, jax.random.fold_in(own_key, 3), *heavy), -most, most).astype(kind)


def setup_inputs(seed: int = 0) -> dict:
    splits = jax.random.split(jax.random.key(seed), 6)
    return {
        "proj": normal_values(splits[0], (SEQUENCE_LENGTH, 3, MODEL_DIMENSION), 1.0, 6.0, ((0, 32), (2, 8))),
        "cotangent": normal_values(splits[1], (SEQUENCE_LENGTH, MODEL_DIMENSION), 1.0, 6.0, ((0, 32), (1, 8))),
        "out_weight": gaussian_with(splits[2], (MODEL_DIMENSION, MODEL_DIMENSION), MODEL_DIMENSION ** -0.5, 0.125, ((0, 32), (1, 8)), (1, 0, 32, 2.75)),
        "short_weight": normal_values(splits[3], (TAPS, 3, MODEL_DIMENSION), TAPS ** -0.5, 2.0, ((2, 8),), jnp.float32),
        "long_filter": draw_long_filter(jax.random.fold_in(splits[5], 71), 0),
    }


def reference(proj, cotangent, out_weight, short_weight, long_filter):
    length = proj.shape[0]
    model_width = out_weight.shape[0]
    taps_count = short_weight.shape[0]
    rim_rows = taps_count - 1
    group_width = model_width // N_TP
    padded = jnp.pad(proj.astype(jnp.float32), ((rim_rows, 0), (0, 0), (0, 0)))
    primed = jnp.zeros(proj.shape, jnp.float32)
    for offset in range(taps_count):
        primed = primed + short_weight[offset][None] * padded[rim_rows - offset:rim_rows - offset + length]
    primed = primed.astype(jnp.bfloat16)
    query_conv = primed[:, 0]
    keys_conv = primed[:, 1]
    value_conv = primed[:, 2]
    gated_input = (keys_conv.astype(jnp.float32) * value_conv.astype(jnp.float32)).astype(jnp.bfloat16)
    summed = jnp.zeros((length, model_width), jnp.float32)
    for group_index in range(N_TP):
        start_col = group_index * group_width
        section = jnp.dot(cotangent[:, start_col:start_col + group_width],
                          out_weight[:, start_col:start_col + group_width].T,
                          preferred_element_type=jnp.float32)
        rounded = lax.optimization_barrier(section.astype(jnp.bfloat16))
        summed = summed + rounded.astype(jnp.float32)
    grad_out = summed.astype(jnp.bfloat16)
    block_count = model_width // 128

    def to_blocks(array):
        return array.reshape(length, block_count, 128).transpose(1, 0, 2)

    def from_blocks(array):
        return array.transpose(1, 0, 2).reshape(length, model_width)

    def long_block(operands):
        gated_block, filter_block, grad_block, query_block = operands
        fft_len = 2 * length
        gated_spec = jnp.fft.rfft(gated_block.astype(jnp.float32), n=fft_len, axis=0)
        filter_spec = jnp.fft.rfft(filter_block.astype(jnp.float32), n=fft_len, axis=0)
        conv_block = jnp.fft.irfft(gated_spec * filter_spec, n=fft_len, axis=0)[:length].astype(jnp.bfloat16)
        grad_query = (grad_block.astype(jnp.float32) * conv_block.astype(jnp.float32)).astype(jnp.bfloat16)
        grad_conv = (grad_block.astype(jnp.float32) * query_block.astype(jnp.float32)).astype(jnp.bfloat16)
        grad_spec = jnp.fft.rfft(grad_conv.astype(jnp.float32), n=fft_len, axis=0)
        gated_grad = jnp.fft.irfft(grad_spec * jnp.conj(filter_spec), n=fft_len, axis=0)[:length].astype(jnp.bfloat16)
        filter_grad = jnp.fft.irfft(grad_spec * jnp.conj(gated_spec), n=fft_len, axis=0)[:length].astype(jnp.float32)
        return grad_query, gated_grad, filter_grad

    grad_query, gated_grad, filter_grad = lax.map(
        long_block, (to_blocks(gated_input), to_blocks(long_filter), to_blocks(grad_out), to_blocks(query_conv)))
    grad_query = from_blocks(grad_query)
    gated_grad = from_blocks(gated_grad)
    grad_filter = from_blocks(filter_grad)
    grad_keys = (gated_grad.astype(jnp.float32) * value_conv.astype(jnp.float32)).astype(jnp.bfloat16)
    grad_value = (gated_grad.astype(jnp.float32) * keys_conv.astype(jnp.float32)).astype(jnp.bfloat16)
    grad_primed = jnp.stack([grad_query, grad_keys, grad_value], axis=1)
    grad_wide = grad_primed.astype(jnp.float32)
    trailing = jnp.pad(grad_wide, ((0, rim_rows), (0, 0), (0, 0)))
    grad_sum = jnp.zeros(proj.shape, jnp.float32)
    for offset in range(taps_count):
        grad_sum = grad_sum + short_weight[offset][None] * trailing[offset:offset + length]
    grad_proj = grad_sum.astype(jnp.bfloat16)
    grad_short = jnp.stack([jnp.sum(grad_wide * padded[rim_rows - offset:rim_rows - offset + length], axis=0)
                            for offset in range(taps_count)])
    return grad_proj, grad_short, grad_filter
```

```python
import math

import jax
import jax.numpy as jnp
from jax import lax
from jax.sharding import PartitionSpec as P

highest = lax.Precision.HIGHEST


def shifted(value, axis, by):
    devices = lax.axis_size(axis)
    pairs = [(i, i + by) for i in range(devices) if 0 <= i + by < devices]
    return lax.ppermute(value, axis, pairs)


def angle_tables(row_count, col_count, modulus):
    row_index = jnp.arange(row_count, dtype=jnp.int32)[:, None]
    col_index = jnp.arange(col_count, dtype=jnp.int32)[None, :]
    phase = (row_index * col_index % modulus).astype(jnp.float32) * (2.0 * math.pi / modulus)
    return (jnp.cos(phase), jnp.sin(phase))


def split_length(length):
    whole_len = 2 * length
    ceiling = 1 << whole_len.bit_length() // 2 - 1
    first_len = 2 * math.gcd(length, ceiling)
    return (first_len, whole_len // first_len)


def spectrum(columns):
    length, channels = columns.shape
    first_len, second_len = split_length(length)
    lower_half = first_len // 2
    whole_len = first_len * second_len
    values = columns.astype(jnp.float32).reshape(lower_half, second_len * channels)
    cos_first, sin_first = angle_tables(first_len, lower_half, first_len)
    real_one = jnp.dot(cos_first, values, precision=highest).reshape(
        first_len, second_len, channels
    )
    imag_one = -jnp.dot(sin_first, values, precision=highest).reshape(
        first_len, second_len, channels
    )
    twist_cos, twist_sin = angle_tables(first_len, second_len, whole_len)
    twist_cos = twist_cos[:, :, None]
    twist_sin = twist_sin[:, :, None]
    real_two = real_one * twist_cos + imag_one * twist_sin
    imag_two = imag_one * twist_cos - real_one * twist_sin
    cos_second, sin_second = angle_tables(second_len, second_len, second_len)
    real_out = jnp.einsum("amc,ml->alc", real_two, cos_second, precision=highest) + jnp.einsum(
        "amc,ml->alc", imag_two, sin_second, precision=highest
    )
    imag_out = jnp.einsum("amc,ml->alc", imag_two, cos_second, precision=highest) - jnp.einsum(
        "amc,ml->alc", real_two, sin_second, precision=highest
    )
    return (real_out, imag_out)


def signal(real_in, imag_in):
    first_len, second_len, channels = real_in.shape
    lower_half = first_len // 2
    whole_len = first_len * second_len
    cos_second, sin_second = angle_tables(second_len, second_len, second_len)
    real_one = jnp.einsum("alc,lm->amc", real_in, cos_second, precision=highest) - jnp.einsum(
        "alc,lm->amc", imag_in, sin_second, precision=highest
    )
    imag_one = jnp.einsum("alc,lm->amc", real_in, sin_second, precision=highest) + jnp.einsum(
        "alc,lm->amc", imag_in, cos_second, precision=highest
    )
    twist_cos, twist_sin = angle_tables(first_len, second_len, whole_len)
    twist_cos = twist_cos[:, :, None]
    twist_sin = twist_sin[:, :, None]
    real_two = real_one * twist_cos - imag_one * twist_sin
    imag_two = real_one * twist_sin + imag_one * twist_cos
    cos_first, sin_first = angle_tables(lower_half, first_len, first_len)
    merged = jnp.dot(
        cos_first, real_two.reshape(first_len, second_len * channels), precision=highest
    ) - jnp.dot(sin_first, imag_two.reshape(first_len, second_len * channels), precision=highest)
    return merged.reshape(lower_half * second_len, channels) / whole_len


def complex_product(left_real, left_imag, right_real, right_imag):
    return (
        left_real * right_real - left_imag * right_imag,
        left_real * right_imag + left_imag * right_real,
    )


def conj_product(left_real, left_imag, right_real, right_imag):
    return (
        left_real * right_real + left_imag * right_imag,
        left_imag * right_real - left_real * right_imag,
    )


def times_bf16(left_array, right_array):
    return (left_array.astype(jnp.float32) * right_array.astype(jnp.float32)).astype(jnp.bfloat16)


def body(proj, cotangent, out_weight, short_weight, long_filter):
    tok_rows = proj.shape[0]
    channels = proj.shape[2]
    taps_count = short_weight.shape[0]
    rim_rows = taps_count - 1
    partial_value = lax.dot_general(
        cotangent,
        lax.all_gather(out_weight, "seq", axis=0, tiled=True),
        (((1,), (1,)), ((), ())),
        preferred_element_type=jnp.float32,
    )
    grad_out = lax.psum_scatter(
        partial_value.astype(jnp.bfloat16), "tp", scatter_dimension=1, tiled=True
    )
    lower_rows = shifted(proj[tok_rows - rim_rows :], "seq", 1)
    extended = jnp.concatenate([lower_rows, proj], axis=0)
    primed = short_weight[0] * extended[rim_rows : rim_rows + tok_rows]
    for offset in range(1, taps_count):
        primed = (
            primed
            + short_weight[offset] * extended[rim_rows - offset : rim_rows - offset + tok_rows]
        )
    primed = primed.astype(jnp.bfloat16)
    query_conv = primed[:, 0]
    keys_conv = primed[:, 1]
    value_conv = primed[:, 2]
    gated_input = times_bf16(keys_conv, value_conv)
    filter_cols = lax.all_to_all(
        long_filter.astype(jnp.bfloat16), "seq", split_axis=1, concat_axis=0, tiled=True
    ).astype(long_filter.dtype)
    filter_real, filter_imag = spectrum(filter_cols)
    gated_cols = lax.all_to_all(gated_input, "seq", split_axis=1, concat_axis=0, tiled=True)
    gated_real, gated_imag = spectrum(gated_cols)
    conv_cols = signal(*complex_product(gated_real, gated_imag, filter_real, filter_imag)).astype(
        jnp.bfloat16
    )
    conv_out = lax.all_to_all(conv_cols, "seq", split_axis=0, concat_axis=1, tiled=True)
    grad_query = times_bf16(grad_out, conv_out)
    grad_conv = times_bf16(grad_out, query_conv)
    grad_cols = lax.all_to_all(grad_conv, "seq", split_axis=1, concat_axis=0, tiled=True)
    grad_real, grad_imag = spectrum(grad_cols)
    gated_grad_cols = signal(*conj_product(grad_real, grad_imag, filter_real, filter_imag)).astype(
        jnp.bfloat16
    )
    filter_grad_cols = signal(*conj_product(grad_real, grad_imag, gated_real, gated_imag))
    gated_grad = lax.all_to_all(gated_grad_cols, "seq", split_axis=0, concat_axis=1, tiled=True)
    grad_filter = lax.all_to_all(
        filter_grad_cols.astype(jnp.bfloat16), "seq", split_axis=0, concat_axis=1, tiled=True
    ).astype(filter_grad_cols.dtype)
    grad_keys = times_bf16(gated_grad, value_conv)
    grad_value = times_bf16(gated_grad, keys_conv)
    grad_primed = jnp.stack([grad_query, grad_keys, grad_value], axis=1)
    next_rows = shifted(grad_primed[:rim_rows], "seq", -1)
    trailing = jnp.concatenate([grad_primed, next_rows], axis=0)
    grad_sum = short_weight[0] * trailing[0:tok_rows]
    for offset in range(1, taps_count):
        grad_sum = grad_sum + short_weight[offset] * trailing[offset : offset + tok_rows]
    grad_proj = grad_sum.astype(jnp.bfloat16)
    grad_wide = grad_primed.astype(jnp.float32)
    local_short = jnp.stack(
        [
            jnp.sum(
                grad_wide
                * extended[rim_rows - offset : rim_rows - offset + tok_rows].astype(jnp.float32),
                axis=0,
            )
            for offset in range(taps_count)
        ]
    )
    short_shape = local_short.shape
    grad_short = lax.psum(local_short.reshape(-1, channels), "seq").reshape(short_shape)
    return (grad_proj, grad_short, grad_filter)


def solution(mesh):
    in_specs = (
        P("seq", None, "tp"),
        P("seq", "tp"),
        P("seq", "tp"),
        P(None, None, "tp"),
        P("seq", "tp"),
    )
    out_specs = (P("seq", None, "tp"), P(None, None, "tp"), P("seq", "tp"))
    return jax.shard_map(body, mesh=mesh, in_specs=in_specs, out_specs=out_specs, check_vma=False)
```

```python
import math

import jax
import jax.numpy as jnp
from jax import lax
from jax.sharding import PartitionSpec as P

highest = lax.Precision.HIGHEST


def shifted(value, axis, by):
    devices = lax.axis_size(axis)
    pairs = [(i, i + by) for i in range(devices) if 0 <= i + by < devices]
    return lax.ppermute(value, axis, pairs)


def angle_tables(row_count, col_count, modulus):
    row_index = jnp.arange(row_count, dtype=jnp.int32)[:, None]
    col_index = jnp.arange(col_count, dtype=jnp.int32)[None, :]
    phase = (row_index * col_index % modulus).astype(jnp.float32) * (2.0 * math.pi / modulus)
    return (jnp.cos(phase), jnp.sin(phase))


def split_length(length):
    whole_len = 2 * length
    ceiling = 1 << whole_len.bit_length() // 2 - 1
    first_len = 2 * math.gcd(length, ceiling)
    return (first_len, whole_len // first_len)


def spectrum(columns):
    length, channels = columns.shape
    first_len, second_len = split_length(length)
    lower_half = first_len // 2
    whole_len = first_len * second_len
    values = columns.astype(jnp.float32).reshape(lower_half, second_len * channels)
    cos_first, sin_first = angle_tables(first_len, lower_half, first_len)
    real_one = jnp.dot(cos_first, values, precision=highest).reshape(
        first_len, second_len, channels
    )
    imag_one = -jnp.dot(sin_first, values, precision=highest).reshape(
        first_len, second_len, channels
    )
    twist_cos, twist_sin = angle_tables(first_len, second_len, whole_len)
    twist_cos = twist_cos[:, :, None]
    twist_sin = twist_sin[:, :, None]
    real_two = real_one * twist_cos + imag_one * twist_sin
    imag_two = imag_one * twist_cos - real_one * twist_sin
    cos_second, sin_second = angle_tables(second_len, second_len, second_len)
    real_out = jnp.einsum("amc,ml->alc", real_two, cos_second, precision=highest) + jnp.einsum(
        "amc,ml->alc", imag_two, sin_second, precision=highest
    )
    imag_out = jnp.einsum("amc,ml->alc", imag_two, cos_second, precision=highest) - jnp.einsum(
        "amc,ml->alc", real_two, sin_second, precision=highest
    )
    return (real_out, imag_out)


def signal(real_in, imag_in):
    first_len, second_len, channels = real_in.shape
    lower_half = first_len // 2
    whole_len = first_len * second_len
    cos_second, sin_second = angle_tables(second_len, second_len, second_len)
    real_one = jnp.einsum("alc,lm->amc", real_in, cos_second, precision=highest) - jnp.einsum(
        "alc,lm->amc", imag_in, sin_second, precision=highest
    )
    imag_one = jnp.einsum("alc,lm->amc", real_in, sin_second, precision=highest) + jnp.einsum(
        "alc,lm->amc", imag_in, cos_second, precision=highest
    )
    twist_cos, twist_sin = angle_tables(first_len, second_len, whole_len)
    twist_cos = twist_cos[:, :, None]
    twist_sin = twist_sin[:, :, None]
    real_two = real_one * twist_cos - imag_one * twist_sin
    imag_two = real_one * twist_sin + imag_one * twist_cos
    cos_first, sin_first = angle_tables(lower_half, first_len, first_len)
    merged = jnp.dot(
        cos_first, real_two.reshape(first_len, second_len * channels), precision=highest
    ) - jnp.dot(sin_first, imag_two.reshape(first_len, second_len * channels), precision=highest)
    return merged.reshape(lower_half * second_len, channels) / whole_len


def complex_product(left_real, left_imag, right_real, right_imag):
    return (
        left_real * right_real - left_imag * right_imag,
        left_real * right_imag + left_imag * right_real,
    )


def conj_product(left_real, left_imag, right_real, right_imag):
    return (
        left_real * right_real + left_imag * right_imag,
        left_imag * right_real - left_real * right_imag,
    )


def times_bf16(left_array, right_array):
    return (left_array.astype(jnp.float32) * right_array.astype(jnp.float32)).astype(jnp.bfloat16)


def output_grad(cotangent, out_weight):
    weight_rows = lax.all_gather(out_weight, "lo", axis=0, tiled=True)
    token_rows = lax.all_gather(cotangent, "hi", axis=0, tiled=True)
    partial_value = lax.dot_general(
        token_rows,
        weight_rows,
        (((1,), (1,)), ((), ())),
        preferred_element_type=jnp.float32,
    ).astype(jnp.bfloat16)
    summed = lax.psum_scatter(partial_value, "tp", scatter_dimension=0, tiled=True)
    hi_count = lax.axis_size("hi")
    tp_count = lax.axis_size("tp")
    pairs = [
        (row * tp_count + col, col * tp_count + row)
        for row in range(hi_count)
        for col in range(tp_count)
    ]
    return lax.ppermute(summed, ("hi", "tp"), pairs)


def butterfly_sum(value, axis):
    devices = lax.axis_size(axis)
    stride = 1
    while stride < devices:
        value = value + lax.ppermute(value, axis, [(i, i ^ stride) for i in range(devices)])
        stride *= 2
    return value


def body(proj, grad_out, short_weight, long_filter):
    tok_rows = proj.shape[0]
    channels = proj.shape[2]
    taps_count = short_weight.shape[0]
    rim_rows = taps_count - 1
    lower_rows = shifted(proj[tok_rows - rim_rows :], "seq", 1)
    extended = jnp.concatenate([lower_rows, proj], axis=0)
    primed = short_weight[0] * extended[rim_rows : rim_rows + tok_rows]
    for offset in range(1, taps_count):
        primed = (
            primed
            + short_weight[offset] * extended[rim_rows - offset : rim_rows - offset + tok_rows]
        )
    primed = primed.astype(jnp.bfloat16)
    query_conv = primed[:, 0]
    keys_conv = primed[:, 1]
    value_conv = primed[:, 2]
    gated_input = times_bf16(keys_conv, value_conv)
    filter_cols = lax.all_to_all(
        long_filter.astype(jnp.bfloat16), "seq", split_axis=1, concat_axis=0, tiled=True
    ).astype(long_filter.dtype)
    filter_real, filter_imag = spectrum(filter_cols)
    gated_cols = lax.all_to_all(gated_input, "seq", split_axis=1, concat_axis=0, tiled=True)
    gated_real, gated_imag = spectrum(gated_cols)
    conv_cols = signal(*complex_product(gated_real, gated_imag, filter_real, filter_imag)).astype(
        jnp.bfloat16
    )
    conv_out = lax.all_to_all(conv_cols, "seq", split_axis=0, concat_axis=1, tiled=True)
    grad_query = times_bf16(grad_out, conv_out)
    grad_conv = times_bf16(grad_out, query_conv)
    grad_cols = lax.all_to_all(grad_conv, "seq", split_axis=1, concat_axis=0, tiled=True)
    grad_real, grad_imag = spectrum(grad_cols)
    gated_grad_cols = signal(*conj_product(grad_real, grad_imag, filter_real, filter_imag)).astype(
        jnp.bfloat16
    )
    filter_grad_cols = signal(*conj_product(grad_real, grad_imag, gated_real, gated_imag))
    gated_grad = lax.all_to_all(gated_grad_cols, "seq", split_axis=0, concat_axis=1, tiled=True)
    grad_filter = lax.all_to_all(
        filter_grad_cols.astype(jnp.bfloat16), "seq", split_axis=0, concat_axis=1, tiled=True
    ).astype(filter_grad_cols.dtype)
    grad_keys = times_bf16(gated_grad, value_conv)
    grad_value = times_bf16(gated_grad, keys_conv)
    grad_primed = jnp.stack([grad_query, grad_keys, grad_value], axis=1)
    next_rows = shifted(grad_primed[:rim_rows], "seq", -1)
    trailing = jnp.concatenate([grad_primed, next_rows], axis=0)
    grad_sum = short_weight[0] * trailing[0:tok_rows]
    for offset in range(1, taps_count):
        grad_sum = grad_sum + short_weight[offset] * trailing[offset : offset + tok_rows]
    grad_proj = grad_sum.astype(jnp.bfloat16)
    grad_wide = grad_primed.astype(jnp.float32)
    local_short = jnp.stack(
        [
            jnp.sum(
                grad_wide
                * extended[rim_rows - offset : rim_rows - offset + tok_rows].astype(jnp.float32),
                axis=0,
            )
            for offset in range(taps_count)
        ]
    )
    grad_short = butterfly_sum(local_short, "seq")
    return (grad_proj, grad_short, grad_filter)


def solution(mesh):
    seq_count = mesh.shape["seq"]
    tp_count = mesh.shape["tp"]
    split_mesh = jax.sharding.Mesh(
        mesh.devices.reshape(tp_count, seq_count // tp_count, tp_count), ("hi", "lo", "tp")
    )
    grad_out_fn = jax.shard_map(
        output_grad,
        mesh=split_mesh,
        in_specs=(P(("hi", "lo"), "tp"), P(("hi", "lo"), "tp")),
        out_specs=P(("hi", "lo"), "tp"),
        check_vma=False,
    )
    in_specs = (
        P("seq", None, "tp"),
        P("seq", "tp"),
        P(None, None, "tp"),
        P("seq", "tp"),
    )
    out_specs = (P("seq", None, "tp"), P(None, None, "tp"), P("seq", "tp"))
    body_fn = jax.shard_map(body, mesh=mesh, in_specs=in_specs, out_specs=out_specs, check_vma=False)

    def run(proj, cotangent, out_weight, short_weight, long_filter):
        grad_out = grad_out_fn(cotangent, out_weight)
        return body_fn(proj, grad_out, short_weight, long_filter)

    return run
```

```python
import math

import jax
import jax.numpy as jnp
from jax import lax
from jax.sharding import PartitionSpec as P

highest = lax.Precision.HIGHEST


def shifted(value, axis, by):
    devices = lax.axis_size(axis)
    pairs = [(i, i + by) for i in range(devices) if 0 <= i + by < devices]
    return lax.ppermute(value, axis, pairs)


def angle_tables(row_count, col_count, modulus):
    row_index = jnp.arange(row_count, dtype=jnp.int32)[:, None]
    col_index = jnp.arange(col_count, dtype=jnp.int32)[None, :]
    phase = (row_index * col_index % modulus).astype(jnp.float32) * (2.0 * math.pi / modulus)
    return (jnp.cos(phase), jnp.sin(phase))


def split_length(length):
    whole_len = 2 * length
    ceiling = 1 << whole_len.bit_length() // 2 - 1
    first_len = 2 * math.gcd(length, ceiling)
    return (first_len, whole_len // first_len)


def spectrum(columns):
    length, channels = columns.shape
    first_len, second_len = split_length(length)
    lower_half = first_len // 2
    whole_len = first_len * second_len
    values = columns.astype(jnp.float32).reshape(lower_half, second_len * channels)
    cos_first, sin_first = angle_tables(first_len, lower_half, first_len)
    real_one = jnp.dot(cos_first, values, precision=highest).reshape(
        first_len, second_len, channels
    )
    imag_one = -jnp.dot(sin_first, values, precision=highest).reshape(
        first_len, second_len, channels
    )
    twist_cos, twist_sin = angle_tables(first_len, second_len, whole_len)
    twist_cos = twist_cos[:, :, None]
    twist_sin = twist_sin[:, :, None]
    real_two = real_one * twist_cos + imag_one * twist_sin
    imag_two = imag_one * twist_cos - real_one * twist_sin
    cos_second, sin_second = angle_tables(second_len, second_len, second_len)
    real_out = jnp.einsum("amc,ml->alc", real_two, cos_second, precision=highest) + jnp.einsum(
        "amc,ml->alc", imag_two, sin_second, precision=highest
    )
    imag_out = jnp.einsum("amc,ml->alc", imag_two, cos_second, precision=highest) - jnp.einsum(
        "amc,ml->alc", real_two, sin_second, precision=highest
    )
    return (real_out, imag_out)


def signal(real_in, imag_in):
    first_len, second_len, channels = real_in.shape
    lower_half = first_len // 2
    whole_len = first_len * second_len
    cos_second, sin_second = angle_tables(second_len, second_len, second_len)
    real_one = jnp.einsum("alc,lm->amc", real_in, cos_second, precision=highest) - jnp.einsum(
        "alc,lm->amc", imag_in, sin_second, precision=highest
    )
    imag_one = jnp.einsum("alc,lm->amc", real_in, sin_second, precision=highest) + jnp.einsum(
        "alc,lm->amc", imag_in, cos_second, precision=highest
    )
    twist_cos, twist_sin = angle_tables(first_len, second_len, whole_len)
    twist_cos = twist_cos[:, :, None]
    twist_sin = twist_sin[:, :, None]
    real_two = real_one * twist_cos - imag_one * twist_sin
    imag_two = real_one * twist_sin + imag_one * twist_cos
    cos_first, sin_first = angle_tables(lower_half, first_len, first_len)
    merged = jnp.dot(
        cos_first, real_two.reshape(first_len, second_len * channels), precision=highest
    ) - jnp.dot(sin_first, imag_two.reshape(first_len, second_len * channels), precision=highest)
    return merged.reshape(lower_half * second_len, channels) / whole_len


def complex_product(left_real, left_imag, right_real, right_imag):
    return (
        left_real * right_real - left_imag * right_imag,
        left_real * right_imag + left_imag * right_real,
    )


def conj_product(left_real, left_imag, right_real, right_imag):
    return (
        left_real * right_real + left_imag * right_imag,
        left_imag * right_real - left_real * right_imag,
    )


def times_bf16(left_array, right_array):
    return (left_array.astype(jnp.float32) * right_array.astype(jnp.float32)).astype(jnp.bfloat16)


def gather_by_permutes(value, axis):
    devices = lax.axis_size(axis)
    parts = [value] + [
        lax.ppermute(value, axis, [(i, (i - step) % devices) for i in range(devices)])
        for step in range(1, devices)
    ]
    stacked = jnp.roll(jnp.stack(parts), lax.axis_index(axis), axis=0)
    return stacked.reshape((-1,) + value.shape[1:])


def output_grad(cotangent, out_weight):
    weight_rows = gather_by_permutes(out_weight, "lo")
    token_rows = gather_by_permutes(cotangent, "hi")
    partial_value = lax.dot_general(
        token_rows,
        weight_rows,
        (((1,), (1,)), ((), ())),
        preferred_element_type=jnp.float32,
    ).astype(jnp.bfloat16)
    hi_count = lax.axis_size("hi")
    tp_count = lax.axis_size("tp")
    chunks = partial_value.reshape((hi_count, -1) + partial_value.shape[1:])
    chunks = jnp.roll(chunks, -lax.axis_index("tp"), axis=0)
    total = None
    for step in range(hi_count):
        pairs = [
            (row * tp_count + col, ((col + step) % hi_count) * tp_count + row)
            for row in range(hi_count)
            for col in range(tp_count)
        ]
        moved = lax.ppermute(chunks[step], ("hi", "tp"), pairs).astype(jnp.float32)
        total = moved if total is None else total + moved
    return total.astype(jnp.bfloat16)


def butterfly_sum(value, axis):
    devices = lax.axis_size(axis)
    stride = 1
    while stride < devices:
        value = value + lax.ppermute(value, axis, [(i, i ^ stride) for i in range(devices)])
        stride *= 2
    return value


def body(proj, grad_out, short_weight, long_filter):
    tok_rows = proj.shape[0]
    channels = proj.shape[2]
    taps_count = short_weight.shape[0]
    rim_rows = taps_count - 1
    lower_rows = shifted(proj[tok_rows - rim_rows :], "seq", 1)
    extended = jnp.concatenate([lower_rows, proj], axis=0)
    primed = short_weight[0] * extended[rim_rows : rim_rows + tok_rows]
    for offset in range(1, taps_count):
        primed = (
            primed
            + short_weight[offset] * extended[rim_rows - offset : rim_rows - offset + tok_rows]
        )
    primed = primed.astype(jnp.bfloat16)
    query_conv = primed[:, 0]
    keys_conv = primed[:, 1]
    value_conv = primed[:, 2]
    gated_input = times_bf16(keys_conv, value_conv)
    filter_cols = lax.all_to_all(
        long_filter.astype(jnp.bfloat16), "seq", split_axis=1, concat_axis=0, tiled=True
    ).astype(long_filter.dtype)
    filter_real, filter_imag = spectrum(filter_cols)
    gated_cols = lax.all_to_all(gated_input, "seq", split_axis=1, concat_axis=0, tiled=True)
    gated_real, gated_imag = spectrum(gated_cols)
    conv_cols = signal(*complex_product(gated_real, gated_imag, filter_real, filter_imag)).astype(
        jnp.bfloat16
    )
    conv_out = lax.all_to_all(conv_cols, "seq", split_axis=0, concat_axis=1, tiled=True)
    grad_query = times_bf16(grad_out, conv_out)
    grad_conv = times_bf16(grad_out, query_conv)
    grad_cols = lax.all_to_all(grad_conv, "seq", split_axis=1, concat_axis=0, tiled=True)
    grad_real, grad_imag = spectrum(grad_cols)
    gated_grad_cols = signal(*conj_product(grad_real, grad_imag, filter_real, filter_imag)).astype(
        jnp.bfloat16
    )
    filter_grad_cols = signal(*conj_product(grad_real, grad_imag, gated_real, gated_imag))
    gated_grad = lax.all_to_all(gated_grad_cols, "seq", split_axis=0, concat_axis=1, tiled=True)
    grad_filter = lax.all_to_all(
        filter_grad_cols.astype(jnp.bfloat16), "seq", split_axis=0, concat_axis=1, tiled=True
    ).astype(filter_grad_cols.dtype)
    grad_keys = times_bf16(gated_grad, value_conv)
    grad_value = times_bf16(gated_grad, keys_conv)
    grad_primed = jnp.stack([grad_query, grad_keys, grad_value], axis=1)
    next_rows = shifted(grad_primed[:rim_rows], "seq", -1)
    trailing = jnp.concatenate([grad_primed, next_rows], axis=0)
    grad_sum = short_weight[0] * trailing[0:tok_rows]
    for offset in range(1, taps_count):
        grad_sum = grad_sum + short_weight[offset] * trailing[offset : offset + tok_rows]
    grad_proj = grad_sum.astype(jnp.bfloat16)
    grad_wide = grad_primed.astype(jnp.float32)
    local_short = jnp.stack(
        [
            jnp.sum(
                grad_wide
                * extended[rim_rows - offset : rim_rows - offset + tok_rows].astype(jnp.float32),
                axis=0,
            )
            for offset in range(taps_count)
        ]
    )
    grad_short = butterfly_sum(local_short, "seq")
    return (grad_proj, grad_short, grad_filter)


def solution(mesh):
    seq_count = mesh.shape["seq"]
    tp_count = mesh.shape["tp"]
    split_mesh = jax.sharding.Mesh(
        mesh.devices.reshape(tp_count, seq_count // tp_count, tp_count), ("hi", "lo", "tp")
    )
    grad_out_fn = jax.shard_map(
        output_grad,
        mesh=split_mesh,
        in_specs=(P(("hi", "lo"), "tp"), P(("hi", "lo"), "tp")),
        out_specs=P(("hi", "lo"), "tp"),
        check_vma=False,
    )
    in_specs = (
        P("seq", None, "tp"),
        P("seq", "tp"),
        P(None, None, "tp"),
        P("seq", "tp"),
    )
    out_specs = (P("seq", None, "tp"), P(None, None, "tp"), P("seq", "tp"))
    body_fn = jax.shard_map(body, mesh=mesh, in_specs=in_specs, out_specs=out_specs, check_vma=False)

    def run(proj, cotangent, out_weight, short_weight, long_filter):
        grad_out = grad_out_fn(cotangent, out_weight)
        return body_fn(proj, grad_out, short_weight, long_filter)

    return run
```

```python
import math

import jax
import jax.numpy as jnp
from jax import lax
from jax.sharding import PartitionSpec as P

highest = lax.Precision.HIGHEST
SEQ = ("hi", "lo")


def shifted(value, axis, by):
    devices = lax.axis_size(axis)
    pairs = [(i, i + by) for i in range(devices) if 0 <= i + by < devices]
    return lax.ppermute(value, axis, pairs)


def angle_tables(row_count, col_count, modulus):
    row_index = jnp.arange(row_count, dtype=jnp.int32)[:, None]
    col_index = jnp.arange(col_count, dtype=jnp.int32)[None, :]
    phase = (row_index * col_index % modulus).astype(jnp.float32) * (2.0 * math.pi / modulus)
    return (jnp.cos(phase), jnp.sin(phase))


def split_length(length):
    whole_len = 2 * length
    ceiling = 1 << whole_len.bit_length() // 2 - 1
    first_len = 2 * math.gcd(length, ceiling)
    return (first_len, whole_len // first_len)


def spectrum(columns):
    length, channels = columns.shape
    first_len, second_len = split_length(length)
    lower_half = first_len // 2
    whole_len = first_len * second_len
    values = columns.astype(jnp.float32).reshape(lower_half, second_len * channels)
    cos_first, sin_first = angle_tables(first_len, lower_half, first_len)
    real_one = jnp.dot(cos_first, values, precision=highest).reshape(
        first_len, second_len, channels
    )
    imag_one = -jnp.dot(sin_first, values, precision=highest).reshape(
        first_len, second_len, channels
    )
    twist_cos, twist_sin = angle_tables(first_len, second_len, whole_len)
    twist_cos = twist_cos[:, :, None]
    twist_sin = twist_sin[:, :, None]
    real_two = real_one * twist_cos + imag_one * twist_sin
    imag_two = imag_one * twist_cos - real_one * twist_sin
    cos_second, sin_second = angle_tables(second_len, second_len, second_len)
    real_out = jnp.einsum("amc,ml->alc", real_two, cos_second, precision=highest) + jnp.einsum(
        "amc,ml->alc", imag_two, sin_second, precision=highest
    )
    imag_out = jnp.einsum("amc,ml->alc", imag_two, cos_second, precision=highest) - jnp.einsum(
        "amc,ml->alc", real_two, sin_second, precision=highest
    )
    return (real_out, imag_out)


def signal(real_in, imag_in):
    first_len, second_len, channels = real_in.shape
    lower_half = first_len // 2
    whole_len = first_len * second_len
    cos_second, sin_second = angle_tables(second_len, second_len, second_len)
    real_one = jnp.einsum("alc,lm->amc", real_in, cos_second, precision=highest) - jnp.einsum(
        "alc,lm->amc", imag_in, sin_second, precision=highest
    )
    imag_one = jnp.einsum("alc,lm->amc", real_in, sin_second, precision=highest) + jnp.einsum(
        "alc,lm->amc", imag_in, cos_second, precision=highest
    )
    twist_cos, twist_sin = angle_tables(first_len, second_len, whole_len)
    twist_cos = twist_cos[:, :, None]
    twist_sin = twist_sin[:, :, None]
    real_two = real_one * twist_cos - imag_one * twist_sin
    imag_two = real_one * twist_sin + imag_one * twist_cos
    cos_first, sin_first = angle_tables(lower_half, first_len, first_len)
    merged = jnp.dot(
        cos_first, real_two.reshape(first_len, second_len * channels), precision=highest
    ) - jnp.dot(sin_first, imag_two.reshape(first_len, second_len * channels), precision=highest)
    return merged.reshape(lower_half * second_len, channels) / whole_len


def complex_product(left_real, left_imag, right_real, right_imag):
    return (
        left_real * right_real - left_imag * right_imag,
        left_real * right_imag + left_imag * right_real,
    )


def conj_product(left_real, left_imag, right_real, right_imag):
    return (
        left_real * right_real + left_imag * right_imag,
        left_imag * right_real - left_real * right_imag,
    )


def times_bf16(left_array, right_array):
    return (left_array.astype(jnp.float32) * right_array.astype(jnp.float32)).astype(jnp.bfloat16)


def output_grad(cotangent, out_weight, ready):
    weight_rows = lax.all_gather(out_weight, "lo", axis=0, tiled=True)
    token_rows = lax.all_gather(cotangent, "hi", axis=0, tiled=True)
    weight_rows, token_rows, _ = lax.optimization_barrier((weight_rows, token_rows, ready))
    partial_value = lax.dot_general(
        token_rows,
        weight_rows,
        (((1,), (1,)), ((), ())),
        preferred_element_type=jnp.float32,
    ).astype(jnp.bfloat16)
    summed = lax.psum_scatter(partial_value, "tp", scatter_dimension=0, tiled=True)
    hi_count = lax.axis_size("hi")
    tp_count = lax.axis_size("tp")
    pairs = [
        (row * tp_count + col, col * tp_count + row)
        for row in range(hi_count)
        for col in range(tp_count)
    ]
    return lax.ppermute(summed, ("hi", "tp"), pairs)


def butterfly_sum(value, axis):
    devices = lax.axis_size(axis)
    stride = 1
    while stride < devices:
        value = value + lax.ppermute(value, axis, [(i, i ^ stride) for i in range(devices)])
        stride *= 2
    return value


def body(proj, cotangent, out_weight, short_weight, long_filter):
    tok_rows = proj.shape[0]
    channels = proj.shape[2]
    taps_count = short_weight.shape[0]
    rim_rows = taps_count - 1
    lower_rows = shifted(proj[tok_rows - rim_rows :], SEQ, 1)
    extended = jnp.concatenate([lower_rows, proj], axis=0)
    primed = short_weight[0] * extended[rim_rows : rim_rows + tok_rows]
    for offset in range(1, taps_count):
        primed = (
            primed
            + short_weight[offset] * extended[rim_rows - offset : rim_rows - offset + tok_rows]
        )
    primed = primed.astype(jnp.bfloat16)
    query_conv = primed[:, 0]
    keys_conv = primed[:, 1]
    value_conv = primed[:, 2]
    gated_input = times_bf16(keys_conv, value_conv)
    filter_cols = lax.all_to_all(
        long_filter.astype(jnp.bfloat16), SEQ, split_axis=1, concat_axis=0, tiled=True
    ).astype(long_filter.dtype)
    filter_real, filter_imag = spectrum(filter_cols)
    gated_cols = lax.all_to_all(gated_input, SEQ, split_axis=1, concat_axis=0, tiled=True)
    gated_real, gated_imag = spectrum(gated_cols)
    conv_cols = signal(*complex_product(gated_real, gated_imag, filter_real, filter_imag)).astype(
        jnp.bfloat16
    )
    conv_out = lax.all_to_all(conv_cols, SEQ, split_axis=0, concat_axis=1, tiled=True)
    grad_out = output_grad(cotangent, out_weight, conv_out)
    grad_query = times_bf16(grad_out, conv_out)
    grad_conv = times_bf16(grad_out, query_conv)
    grad_cols = lax.all_to_all(grad_conv, SEQ, split_axis=1, concat_axis=0, tiled=True)
    grad_real, grad_imag = spectrum(grad_cols)
    gated_grad_cols = signal(*conj_product(grad_real, grad_imag, filter_real, filter_imag)).astype(
        jnp.bfloat16
    )
    filter_grad_cols = signal(*conj_product(grad_real, grad_imag, gated_real, gated_imag))
    gated_grad = lax.all_to_all(gated_grad_cols, SEQ, split_axis=0, concat_axis=1, tiled=True)
    grad_filter = lax.all_to_all(
        filter_grad_cols.astype(jnp.bfloat16), SEQ, split_axis=0, concat_axis=1, tiled=True
    ).astype(filter_grad_cols.dtype)
    grad_keys = times_bf16(gated_grad, value_conv)
    grad_value = times_bf16(gated_grad, keys_conv)
    grad_primed = jnp.stack([grad_query, grad_keys, grad_value], axis=1)
    next_rows = shifted(grad_primed[:rim_rows], SEQ, -1)
    trailing = jnp.concatenate([grad_primed, next_rows], axis=0)
    grad_sum = short_weight[0] * trailing[0:tok_rows]
    for offset in range(1, taps_count):
        grad_sum = grad_sum + short_weight[offset] * trailing[offset : offset + tok_rows]
    grad_proj = grad_sum.astype(jnp.bfloat16)
    grad_wide = grad_primed.astype(jnp.float32)
    local_short = jnp.stack(
        [
            jnp.sum(
                grad_wide
                * extended[rim_rows - offset : rim_rows - offset + tok_rows].astype(jnp.float32),
                axis=0,
            )
            for offset in range(taps_count)
        ]
    )
    grad_short = butterfly_sum(local_short, SEQ)
    return (grad_proj, grad_short, grad_filter)


def solution(mesh):
    seq_count = mesh.shape["seq"]
    tp_count = mesh.shape["tp"]
    split_mesh = jax.sharding.Mesh(
        mesh.devices.reshape(tp_count, seq_count // tp_count, tp_count), ("hi", "lo", "tp")
    )
    in_specs = (
        P(SEQ, None, "tp"),
        P(SEQ, "tp"),
        P(SEQ, "tp"),
        P(None, None, "tp"),
        P(SEQ, "tp"),
    )
    out_specs = (P(SEQ, None, "tp"), P(None, None, "tp"), P(SEQ, "tp"))
    return jax.shard_map(
        body, mesh=split_mesh, in_specs=in_specs, out_specs=out_specs, check_vma=False
    )
```

```python
import math

import jax
import jax.numpy as jnp
from jax import lax
from jax.sharding import PartitionSpec as P

highest = lax.Precision.HIGHEST
SEQ = ("hi", "lo")


def shifted(value, axis, by):
    devices = lax.axis_size(axis)
    pairs = [(i, i + by) for i in range(devices) if 0 <= i + by < devices]
    return lax.ppermute(value, axis, pairs)


def angle_tables(row_count, col_count, modulus):
    row_index = jnp.arange(row_count, dtype=jnp.int32)[:, None]
    col_index = jnp.arange(col_count, dtype=jnp.int32)[None, :]
    phase = (row_index * col_index % modulus).astype(jnp.float32) * (2.0 * math.pi / modulus)
    return (jnp.cos(phase), jnp.sin(phase))


def split_length(length):
    whole_len = 2 * length
    ceiling = 1 << whole_len.bit_length() // 2 - 1
    first_len = 2 * math.gcd(length, ceiling)
    return (first_len, whole_len // first_len)


def spectrum(columns):
    length, channels = columns.shape
    first_len, second_len = split_length(length)
    lower_half = first_len // 2
    whole_len = first_len * second_len
    values = columns.astype(jnp.float32).reshape(lower_half, second_len * channels)
    cos_first, sin_first = angle_tables(first_len, lower_half, first_len)
    real_one = jnp.dot(cos_first, values, precision=highest).reshape(
        first_len, second_len, channels
    )
    imag_one = -jnp.dot(sin_first, values, precision=highest).reshape(
        first_len, second_len, channels
    )
    twist_cos, twist_sin = angle_tables(first_len, second_len, whole_len)
    twist_cos = twist_cos[:, :, None]
    twist_sin = twist_sin[:, :, None]
    real_two = real_one * twist_cos + imag_one * twist_sin
    imag_two = imag_one * twist_cos - real_one * twist_sin
    cos_second, sin_second = angle_tables(second_len, second_len, second_len)
    real_out = jnp.einsum("amc,ml->alc", real_two, cos_second, precision=highest) + jnp.einsum(
        "amc,ml->alc", imag_two, sin_second, precision=highest
    )
    imag_out = jnp.einsum("amc,ml->alc", imag_two, cos_second, precision=highest) - jnp.einsum(
        "amc,ml->alc", real_two, sin_second, precision=highest
    )
    return (real_out, imag_out)


def signal(real_in, imag_in):
    first_len, second_len, channels = real_in.shape
    lower_half = first_len // 2
    whole_len = first_len * second_len
    cos_second, sin_second = angle_tables(second_len, second_len, second_len)
    real_one = jnp.einsum("alc,lm->amc", real_in, cos_second, precision=highest) - jnp.einsum(
        "alc,lm->amc", imag_in, sin_second, precision=highest
    )
    imag_one = jnp.einsum("alc,lm->amc", real_in, sin_second, precision=highest) + jnp.einsum(
        "alc,lm->amc", imag_in, cos_second, precision=highest
    )
    twist_cos, twist_sin = angle_tables(first_len, second_len, whole_len)
    twist_cos = twist_cos[:, :, None]
    twist_sin = twist_sin[:, :, None]
    real_two = real_one * twist_cos - imag_one * twist_sin
    imag_two = real_one * twist_sin + imag_one * twist_cos
    cos_first, sin_first = angle_tables(lower_half, first_len, first_len)
    merged = jnp.dot(
        cos_first, real_two.reshape(first_len, second_len * channels), precision=highest
    ) - jnp.dot(sin_first, imag_two.reshape(first_len, second_len * channels), precision=highest)
    return merged.reshape(lower_half * second_len, channels) / whole_len


def complex_product(left_real, left_imag, right_real, right_imag):
    return (
        left_real * right_real - left_imag * right_imag,
        left_real * right_imag + left_imag * right_real,
    )


def conj_product(left_real, left_imag, right_real, right_imag):
    return (
        left_real * right_real + left_imag * right_imag,
        left_imag * right_real - left_real * right_imag,
    )


def times_bf16(left_array, right_array):
    return (left_array.astype(jnp.float32) * right_array.astype(jnp.float32)).astype(jnp.bfloat16)


def output_grad(cotangent, out_weight, ready):
    weight_rows = lax.all_gather(out_weight, "lo", axis=0, tiled=True)
    token_rows = lax.all_gather(cotangent, "hi", axis=0, tiled=True)
    weight_rows, token_rows, _ = lax.optimization_barrier((weight_rows, token_rows, ready))
    partial_value = lax.dot_general(
        token_rows,
        weight_rows,
        (((1,), (1,)), ((), ())),
        preferred_element_type=jnp.float32,
    ).astype(jnp.bfloat16)
    tp_parts = lax.axis_size("tp")
    chunks = partial_value.reshape((tp_parts, -1) + partial_value.shape[1:])
    received = lax.all_to_all(chunks, "tp", split_axis=0, concat_axis=0, tiled=True)
    summed = jnp.sum(received.astype(jnp.float32), axis=0).astype(jnp.bfloat16)
    hi_count = lax.axis_size("hi")
    tp_count = lax.axis_size("tp")
    pairs = [
        (row * tp_count + col, col * tp_count + row)
        for row in range(hi_count)
        for col in range(tp_count)
    ]
    return lax.ppermute(summed, ("hi", "tp"), pairs)


def butterfly_sum(value, axis):
    devices = lax.axis_size(axis)
    stride = 1
    while stride < devices:
        value = value + lax.ppermute(value, axis, [(i, i ^ stride) for i in range(devices)])
        stride *= 2
    return value


def body(proj, cotangent, out_weight, short_weight, long_filter):
    tok_rows = proj.shape[0]
    channels = proj.shape[2]
    taps_count = short_weight.shape[0]
    rim_rows = taps_count - 1
    lower_rows = shifted(proj[tok_rows - rim_rows :], SEQ, 1)
    extended = jnp.concatenate([lower_rows, proj], axis=0)
    primed = short_weight[0] * extended[rim_rows : rim_rows + tok_rows]
    for offset in range(1, taps_count):
        primed = (
            primed
            + short_weight[offset] * extended[rim_rows - offset : rim_rows - offset + tok_rows]
        )
    primed = primed.astype(jnp.bfloat16)
    query_conv = primed[:, 0]
    keys_conv = primed[:, 1]
    value_conv = primed[:, 2]
    gated_input = times_bf16(keys_conv, value_conv)
    filter_cols = lax.all_to_all(
        long_filter.astype(jnp.bfloat16), SEQ, split_axis=1, concat_axis=0, tiled=True
    ).astype(long_filter.dtype)
    filter_real, filter_imag = spectrum(filter_cols)
    gated_cols = lax.all_to_all(gated_input, SEQ, split_axis=1, concat_axis=0, tiled=True)
    gated_real, gated_imag = spectrum(gated_cols)
    conv_cols = signal(*complex_product(gated_real, gated_imag, filter_real, filter_imag)).astype(
        jnp.bfloat16
    )
    conv_out = lax.all_to_all(conv_cols, SEQ, split_axis=0, concat_axis=1, tiled=True)
    grad_out = output_grad(cotangent, out_weight, conv_out)
    grad_query = times_bf16(grad_out, conv_out)
    grad_conv = times_bf16(grad_out, query_conv)
    grad_cols = lax.all_to_all(grad_conv, SEQ, split_axis=1, concat_axis=0, tiled=True)
    grad_real, grad_imag = spectrum(grad_cols)
    gated_grad_cols = signal(*conj_product(grad_real, grad_imag, filter_real, filter_imag)).astype(
        jnp.bfloat16
    )
    filter_grad_cols = signal(*conj_product(grad_real, grad_imag, gated_real, gated_imag))
    gated_grad = lax.all_to_all(gated_grad_cols, SEQ, split_axis=0, concat_axis=1, tiled=True)
    grad_filter = lax.all_to_all(
        filter_grad_cols.astype(jnp.bfloat16), SEQ, split_axis=0, concat_axis=1, tiled=True
    ).astype(filter_grad_cols.dtype)
    grad_keys = times_bf16(gated_grad, value_conv)
    grad_value = times_bf16(gated_grad, keys_conv)
    grad_primed = jnp.stack([grad_query, grad_keys, grad_value], axis=1)
    next_rows = shifted(grad_primed[:rim_rows], SEQ, -1)
    trailing = jnp.concatenate([grad_primed, next_rows], axis=0)
    grad_sum = short_weight[0] * trailing[0:tok_rows]
    for offset in range(1, taps_count):
        grad_sum = grad_sum + short_weight[offset] * trailing[offset : offset + tok_rows]
    grad_proj = grad_sum.astype(jnp.bfloat16)
    grad_wide = grad_primed.astype(jnp.float32)
    local_short = jnp.stack(
        [
            jnp.sum(
                grad_wide
                * extended[rim_rows - offset : rim_rows - offset + tok_rows].astype(jnp.float32),
                axis=0,
            )
            for offset in range(taps_count)
        ]
    )
    grad_short = butterfly_sum(local_short, SEQ)
    return (grad_proj, grad_short, grad_filter)


def solution(mesh):
    seq_count = mesh.shape["seq"]
    tp_count = mesh.shape["tp"]
    split_mesh = jax.sharding.Mesh(
        mesh.devices.reshape(tp_count, seq_count // tp_count, tp_count), ("hi", "lo", "tp")
    )
    in_specs = (
        P(SEQ, None, "tp"),
        P(SEQ, "tp"),
        P(SEQ, "tp"),
        P(None, None, "tp"),
        P(SEQ, "tp"),
    )
    out_specs = (P(SEQ, None, "tp"), P(None, None, "tp"), P(SEQ, "tp"))
    return jax.shard_map(
        body, mesh=split_mesh, in_specs=in_specs, out_specs=out_specs, check_vma=False
    )
```

```python
import math

import jax
import jax.numpy as jnp
from jax import lax
from jax.sharding import PartitionSpec as P

highest = lax.Precision.HIGHEST
SEQ = ("hi", "lo")


def shifted(value, axis, by):
    devices = lax.axis_size(axis)
    pairs = [(i, i + by) for i in range(devices) if 0 <= i + by < devices]
    return lax.ppermute(value, axis, pairs)


def angle_tables(row_count, col_count, modulus):
    row_index = jnp.arange(row_count, dtype=jnp.int32)[:, None]
    col_index = jnp.arange(col_count, dtype=jnp.int32)[None, :]
    phase = (row_index * col_index % modulus).astype(jnp.float32) * (2.0 * math.pi / modulus)
    return (jnp.cos(phase), jnp.sin(phase))


def split_length(length):
    whole_len = 2 * length
    ceiling = 1 << whole_len.bit_length() // 2 - 1
    first_len = 2 * math.gcd(length, ceiling)
    return (first_len, whole_len // first_len)


def spectrum(columns):
    length, channels = columns.shape
    first_len, second_len = split_length(length)
    lower_half = first_len // 2
    whole_len = first_len * second_len
    values = columns.astype(jnp.float32).reshape(lower_half, second_len * channels)
    cos_first, sin_first = angle_tables(first_len, lower_half, first_len)
    real_one = jnp.dot(cos_first, values, precision=highest).reshape(
        first_len, second_len, channels
    )
    imag_one = -jnp.dot(sin_first, values, precision=highest).reshape(
        first_len, second_len, channels
    )
    twist_cos, twist_sin = angle_tables(first_len, second_len, whole_len)
    twist_cos = twist_cos[:, :, None]
    twist_sin = twist_sin[:, :, None]
    real_two = real_one * twist_cos + imag_one * twist_sin
    imag_two = imag_one * twist_cos - real_one * twist_sin
    cos_second, sin_second = angle_tables(second_len, second_len, second_len)
    real_out = jnp.einsum("amc,ml->alc", real_two, cos_second, precision=highest) + jnp.einsum(
        "amc,ml->alc", imag_two, sin_second, precision=highest
    )
    imag_out = jnp.einsum("amc,ml->alc", imag_two, cos_second, precision=highest) - jnp.einsum(
        "amc,ml->alc", real_two, sin_second, precision=highest
    )
    return (real_out, imag_out)


def signal(real_in, imag_in):
    first_len, second_len, channels = real_in.shape
    lower_half = first_len // 2
    whole_len = first_len * second_len
    cos_second, sin_second = angle_tables(second_len, second_len, second_len)
    real_one = jnp.einsum("alc,lm->amc", real_in, cos_second, precision=highest) - jnp.einsum(
        "alc,lm->amc", imag_in, sin_second, precision=highest
    )
    imag_one = jnp.einsum("alc,lm->amc", real_in, sin_second, precision=highest) + jnp.einsum(
        "alc,lm->amc", imag_in, cos_second, precision=highest
    )
    twist_cos, twist_sin = angle_tables(first_len, second_len, whole_len)
    twist_cos = twist_cos[:, :, None]
    twist_sin = twist_sin[:, :, None]
    real_two = real_one * twist_cos - imag_one * twist_sin
    imag_two = real_one * twist_sin + imag_one * twist_cos
    cos_first, sin_first = angle_tables(lower_half, first_len, first_len)
    merged = jnp.dot(
        cos_first, real_two.reshape(first_len, second_len * channels), precision=highest
    ) - jnp.dot(sin_first, imag_two.reshape(first_len, second_len * channels), precision=highest)
    return merged.reshape(lower_half * second_len, channels) / whole_len


def complex_product(left_real, left_imag, right_real, right_imag):
    return (
        left_real * right_real - left_imag * right_imag,
        left_real * right_imag + left_imag * right_real,
    )


def conj_product(left_real, left_imag, right_real, right_imag):
    return (
        left_real * right_real + left_imag * right_imag,
        left_imag * right_real - left_real * right_imag,
    )


def times_bf16(left_array, right_array):
    return (left_array.astype(jnp.float32) * right_array.astype(jnp.float32)).astype(jnp.bfloat16)


def output_grad(cotangent, out_weight, ready):
    weight_rows = lax.all_gather(out_weight, "lo", axis=0, tiled=True)
    token_rows = lax.all_gather(cotangent, "hi", axis=0, tiled=True)
    weight_rows, token_rows, _ = lax.optimization_barrier((weight_rows, token_rows, ready))
    partial_value = lax.dot_general(
        token_rows,
        weight_rows,
        (((1,), (1,)), ((), ())),
        preferred_element_type=jnp.float32,
    ).astype(jnp.bfloat16)
    tp_parts = lax.axis_size("tp")
    chunks = partial_value.reshape((tp_parts, -1) + partial_value.shape[1:])
    received = lax.all_to_all(chunks, "tp", split_axis=0, concat_axis=0, tiled=True)
    summed = jnp.sum(received.astype(jnp.float32), axis=0).astype(jnp.bfloat16)
    hi_count = lax.axis_size("hi")
    tp_count = lax.axis_size("tp")
    pairs = [
        (row * tp_count + col, col * tp_count + row)
        for row in range(hi_count)
        for col in range(tp_count)
    ]
    return lax.ppermute(summed, ("hi", "tp"), pairs)


def butterfly_sum(value, axis):
    devices = lax.axis_size(axis)
    stride = 1
    while stride < devices:
        value = value + lax.ppermute(value, axis, [(i, i ^ stride) for i in range(devices)])
        stride *= 2
    return value


def body(proj, cotangent, out_weight, short_weight, long_filter):
    tok_rows = proj.shape[0]
    channels = proj.shape[2]
    taps_count = short_weight.shape[0]
    rim_rows = taps_count - 1
    lower_rows = shifted(proj[tok_rows - rim_rows :], SEQ, 1)
    extended = jnp.concatenate([lower_rows, proj], axis=0)
    primed = short_weight[0] * extended[rim_rows : rim_rows + tok_rows]
    for offset in range(1, taps_count):
        primed = (
            primed
            + short_weight[offset] * extended[rim_rows - offset : rim_rows - offset + tok_rows]
        )
    primed = primed.astype(jnp.bfloat16)
    query_conv = primed[:, 0]
    keys_conv = primed[:, 1]
    value_conv = primed[:, 2]
    gated_input = times_bf16(keys_conv, value_conv)
    both_rows = jnp.stack([long_filter.astype(jnp.bfloat16), gated_input], axis=1)
    both_cols = lax.all_to_all(both_rows, SEQ, split_axis=2, concat_axis=0, tiled=True)
    filter_cols = both_cols[:, 0].astype(long_filter.dtype)
    filter_real, filter_imag = spectrum(filter_cols)
    gated_cols = both_cols[:, 1]
    gated_real, gated_imag = spectrum(gated_cols)
    conv_cols = signal(*complex_product(gated_real, gated_imag, filter_real, filter_imag)).astype(
        jnp.bfloat16
    )
    conv_out = lax.all_to_all(conv_cols, SEQ, split_axis=0, concat_axis=1, tiled=True)
    grad_out = output_grad(cotangent, out_weight, conv_out)
    grad_query = times_bf16(grad_out, conv_out)
    grad_conv = times_bf16(grad_out, query_conv)
    grad_cols = lax.all_to_all(grad_conv, SEQ, split_axis=1, concat_axis=0, tiled=True)
    grad_real, grad_imag = spectrum(grad_cols)
    gated_grad_cols = signal(*conj_product(grad_real, grad_imag, filter_real, filter_imag)).astype(
        jnp.bfloat16
    )
    filter_grad_cols = signal(*conj_product(grad_real, grad_imag, gated_real, gated_imag))
    back_cols = jnp.stack([gated_grad_cols, filter_grad_cols.astype(jnp.bfloat16)], axis=1)
    back_rows = lax.all_to_all(back_cols, SEQ, split_axis=0, concat_axis=2, tiled=True)
    gated_grad = back_rows[:, 0]
    grad_filter = back_rows[:, 1].astype(filter_grad_cols.dtype)
    grad_keys = times_bf16(gated_grad, value_conv)
    grad_value = times_bf16(gated_grad, keys_conv)
    grad_primed = jnp.stack([grad_query, grad_keys, grad_value], axis=1)
    next_rows = shifted(grad_primed[:rim_rows], SEQ, -1)
    trailing = jnp.concatenate([grad_primed, next_rows], axis=0)
    grad_sum = short_weight[0] * trailing[0:tok_rows]
    for offset in range(1, taps_count):
        grad_sum = grad_sum + short_weight[offset] * trailing[offset : offset + tok_rows]
    grad_proj = grad_sum.astype(jnp.bfloat16)
    grad_wide = grad_primed.astype(jnp.float32)
    local_short = jnp.stack(
        [
            jnp.sum(
                grad_wide
                * extended[rim_rows - offset : rim_rows - offset + tok_rows].astype(jnp.float32),
                axis=0,
            )
            for offset in range(taps_count)
        ]
    )
    grad_short = butterfly_sum(local_short, SEQ)
    return (grad_proj, grad_short, grad_filter)


def solution(mesh):
    seq_count = mesh.shape["seq"]
    tp_count = mesh.shape["tp"]
    split_mesh = jax.sharding.Mesh(
        mesh.devices.reshape(tp_count, seq_count // tp_count, tp_count), ("hi", "lo", "tp")
    )
    in_specs = (
        P(SEQ, None, "tp"),
        P(SEQ, "tp"),
        P(SEQ, "tp"),
        P(None, None, "tp"),
        P(SEQ, "tp"),
    )
    out_specs = (P(SEQ, None, "tp"), P(None, None, "tp"), P(SEQ, "tp"))
    return jax.shard_map(
        body, mesh=split_mesh, in_specs=in_specs, out_specs=out_specs, check_vma=False
    )
```

```python
import math

import jax
import jax.numpy as jnp
from jax import lax
from jax.sharding import PartitionSpec as P

highest = lax.Precision.HIGHEST
SEQ = ("hi", "lo")


def shifted(value, axis, by):
    devices = lax.axis_size(axis)
    pairs = [(i, i + by) for i in range(devices) if 0 <= i + by < devices]
    return lax.ppermute(value, axis, pairs)


def angle_tables(row_count, col_count, modulus):
    row_index = jnp.arange(row_count, dtype=jnp.int32)[:, None]
    col_index = jnp.arange(col_count, dtype=jnp.int32)[None, :]
    phase = (row_index * col_index % modulus).astype(jnp.float32) * (2.0 * math.pi / modulus)
    return (jnp.cos(phase), jnp.sin(phase))


def split_length(length):
    whole_len = 2 * length
    ceiling = 1 << whole_len.bit_length() // 2 - 1
    first_len = 2 * math.gcd(length, ceiling)
    return (first_len, whole_len // first_len)


def spectrum(columns):
    length, channels = columns.shape
    first_len, second_len = split_length(length)
    lower_half = first_len // 2
    whole_len = first_len * second_len
    values = columns.astype(jnp.float32).reshape(lower_half, second_len * channels)
    cos_first, sin_first = angle_tables(first_len, lower_half, first_len)
    real_one = jnp.dot(cos_first, values, precision=highest).reshape(
        first_len, second_len, channels
    )
    imag_one = -jnp.dot(sin_first, values, precision=highest).reshape(
        first_len, second_len, channels
    )
    twist_cos, twist_sin = angle_tables(first_len, second_len, whole_len)
    twist_cos = twist_cos[:, :, None]
    twist_sin = twist_sin[:, :, None]
    real_two = real_one * twist_cos + imag_one * twist_sin
    imag_two = imag_one * twist_cos - real_one * twist_sin
    cos_second, sin_second = angle_tables(second_len, second_len, second_len)
    real_out = jnp.einsum("amc,ml->alc", real_two, cos_second, precision=highest) + jnp.einsum(
        "amc,ml->alc", imag_two, sin_second, precision=highest
    )
    imag_out = jnp.einsum("amc,ml->alc", imag_two, cos_second, precision=highest) - jnp.einsum(
        "amc,ml->alc", real_two, sin_second, precision=highest
    )
    return (real_out, imag_out)


def signal(real_in, imag_in):
    first_len, second_len, channels = real_in.shape
    lower_half = first_len // 2
    whole_len = first_len * second_len
    cos_second, sin_second = angle_tables(second_len, second_len, second_len)
    real_one = jnp.einsum("alc,lm->amc", real_in, cos_second, precision=highest) - jnp.einsum(
        "alc,lm->amc", imag_in, sin_second, precision=highest
    )
    imag_one = jnp.einsum("alc,lm->amc", real_in, sin_second, precision=highest) + jnp.einsum(
        "alc,lm->amc", imag_in, cos_second, precision=highest
    )
    twist_cos, twist_sin = angle_tables(first_len, second_len, whole_len)
    twist_cos = twist_cos[:, :, None]
    twist_sin = twist_sin[:, :, None]
    real_two = real_one * twist_cos - imag_one * twist_sin
    imag_two = real_one * twist_sin + imag_one * twist_cos
    cos_first, sin_first = angle_tables(lower_half, first_len, first_len)
    merged = jnp.dot(
        cos_first, real_two.reshape(first_len, second_len * channels), precision=highest
    ) - jnp.dot(sin_first, imag_two.reshape(first_len, second_len * channels), precision=highest)
    return merged.reshape(lower_half * second_len, channels) / whole_len


def complex_product(left_real, left_imag, right_real, right_imag):
    return (
        left_real * right_real - left_imag * right_imag,
        left_real * right_imag + left_imag * right_real,
    )


def conj_product(left_real, left_imag, right_real, right_imag):
    return (
        left_real * right_real + left_imag * right_imag,
        left_imag * right_real - left_real * right_imag,
    )


def times_bf16(left_array, right_array):
    return (left_array.astype(jnp.float32) * right_array.astype(jnp.float32)).astype(jnp.bfloat16)


def transposed(value):
    hi_count = lax.axis_size("hi")
    tp_count = lax.axis_size("tp")
    pairs = [
        (row * tp_count + col, col * tp_count + row)
        for row in range(hi_count)
        for col in range(tp_count)
    ]
    return lax.ppermute(value, ("hi", "tp"), pairs)


def output_grad(cotangent, out_weight, ready):
    weight_rows = lax.all_gather(transposed(out_weight), "lo", axis=0, tiled=True)
    token_rows = lax.all_gather(transposed(cotangent), "tp", axis=0, tiled=True)
    weight_rows, token_rows, ready = lax.optimization_barrier((weight_rows, token_rows, ready))
    partial_value = lax.dot_general(
        token_rows,
        weight_rows,
        (((1,), (1,)), ((), ())),
        preferred_element_type=jnp.float32,
    ).astype(jnp.bfloat16)
    hi_parts = lax.axis_size("hi")
    chunks = partial_value.reshape((hi_parts, -1) + partial_value.shape[1:])
    received = lax.all_to_all(chunks, "hi", split_axis=0, concat_axis=0, tiled=True)
    return jnp.sum(received.astype(jnp.float32), axis=0).astype(jnp.bfloat16), ready


def butterfly_sum(value, axis):
    devices = lax.axis_size(axis)
    stride = 1
    while stride < devices:
        value = value + lax.ppermute(value, axis, [(i, i ^ stride) for i in range(devices)])
        stride *= 2
    return value


def body(proj, cotangent, out_weight, short_weight, long_filter):
    tok_rows = proj.shape[0]
    channels = proj.shape[2]
    taps_count = short_weight.shape[0]
    rim_rows = taps_count - 1
    lower_rows = shifted(proj[tok_rows - rim_rows :], SEQ, 1)
    extended = jnp.concatenate([lower_rows, proj], axis=0)
    primed = short_weight[0] * extended[rim_rows : rim_rows + tok_rows]
    for offset in range(1, taps_count):
        primed = (
            primed
            + short_weight[offset] * extended[rim_rows - offset : rim_rows - offset + tok_rows]
        )
    primed = primed.astype(jnp.bfloat16)
    query_conv = primed[:, 0]
    keys_conv = primed[:, 1]
    value_conv = primed[:, 2]
    gated_input = times_bf16(keys_conv, value_conv)
    filter_cols = lax.all_to_all(
        long_filter.astype(jnp.bfloat16), SEQ, split_axis=1, concat_axis=0, tiled=True
    ).astype(long_filter.dtype)
    filter_real, filter_imag = spectrum(filter_cols)
    gated_cols = lax.all_to_all(gated_input, SEQ, split_axis=1, concat_axis=0, tiled=True)
    gated_real, gated_imag = spectrum(gated_cols)
    conv_cols = signal(*complex_product(gated_real, gated_imag, filter_real, filter_imag)).astype(
        jnp.bfloat16
    )
    conv_out = lax.all_to_all(conv_cols, SEQ, split_axis=0, concat_axis=1, tiled=True)
    grad_out, conv_out = output_grad(cotangent, out_weight, conv_out)
    grad_query = times_bf16(grad_out, conv_out)
    grad_conv = times_bf16(grad_out, query_conv)
    grad_cols = lax.all_to_all(grad_conv, SEQ, split_axis=1, concat_axis=0, tiled=True)
    grad_real, grad_imag = spectrum(grad_cols)
    gated_grad_cols = signal(*conj_product(grad_real, grad_imag, filter_real, filter_imag)).astype(
        jnp.bfloat16
    )
    filter_grad_cols = signal(*conj_product(grad_real, grad_imag, gated_real, gated_imag))
    gated_grad = lax.all_to_all(gated_grad_cols, SEQ, split_axis=0, concat_axis=1, tiled=True)
    grad_filter = lax.all_to_all(
        filter_grad_cols.astype(jnp.bfloat16), SEQ, split_axis=0, concat_axis=1, tiled=True
    ).astype(filter_grad_cols.dtype)
    grad_keys = times_bf16(gated_grad, value_conv)
    grad_value = times_bf16(gated_grad, keys_conv)
    grad_primed = jnp.stack([grad_query, grad_keys, grad_value], axis=1)
    next_rows = shifted(grad_primed[:rim_rows], SEQ, -1)
    trailing = jnp.concatenate([grad_primed, next_rows], axis=0)
    grad_sum = short_weight[0] * trailing[0:tok_rows]
    for offset in range(1, taps_count):
        grad_sum = grad_sum + short_weight[offset] * trailing[offset : offset + tok_rows]
    grad_proj = grad_sum.astype(jnp.bfloat16)
    grad_wide = grad_primed.astype(jnp.float32)
    local_short = jnp.stack(
        [
            jnp.sum(
                grad_wide
                * extended[rim_rows - offset : rim_rows - offset + tok_rows].astype(jnp.float32),
                axis=0,
            )
            for offset in range(taps_count)
        ]
    )
    grad_short = butterfly_sum(local_short, SEQ)
    return (grad_proj, grad_short, grad_filter)


def solution(mesh):
    seq_count = mesh.shape["seq"]
    tp_count = mesh.shape["tp"]
    split_mesh = jax.sharding.Mesh(
        mesh.devices.reshape(tp_count, seq_count // tp_count, tp_count), ("hi", "lo", "tp")
    )
    in_specs = (
        P(SEQ, None, "tp"),
        P(SEQ, "tp"),
        P(SEQ, "tp"),
        P(None, None, "tp"),
        P(SEQ, "tp"),
    )
    out_specs = (P(SEQ, None, "tp"), P(None, None, "tp"), P(SEQ, "tp"))
    return jax.shard_map(
        body, mesh=split_mesh, in_specs=in_specs, out_specs=out_specs, check_vma=False
    )
```

```python
import math

import jax
import jax.numpy as jnp
from jax import lax
from jax.sharding import PartitionSpec as P

highest = lax.Precision.HIGH
SEQ = ("hi", "lo")


def shifted(value, axis, by):
    devices = lax.axis_size(axis)
    pairs = [(i, i + by) for i in range(devices) if 0 <= i + by < devices]
    return lax.ppermute(value, axis, pairs)


def angle_tables(row_count, col_count, modulus):
    row_index = jnp.arange(row_count, dtype=jnp.int32)[:, None]
    col_index = jnp.arange(col_count, dtype=jnp.int32)[None, :]
    phase = (row_index * col_index % modulus).astype(jnp.float32) * (2.0 * math.pi / modulus)
    return (jnp.cos(phase), jnp.sin(phase))


def split_length(length):
    whole_len = 2 * length
    ceiling = 1 << whole_len.bit_length() // 2 - 1
    first_len = 2 * math.gcd(length, ceiling)
    return (first_len, whole_len // first_len)


def spectrum(columns):
    length, channels = columns.shape
    first_len, second_len = split_length(length)
    lower_half = first_len // 2
    whole_len = first_len * second_len
    values = columns.astype(jnp.float32).reshape(lower_half, second_len * channels)
    cos_first, sin_first = angle_tables(first_len, lower_half, first_len)
    real_one = jnp.dot(cos_first, values, precision=highest).reshape(
        first_len, second_len, channels
    )
    imag_one = -jnp.dot(sin_first, values, precision=highest).reshape(
        first_len, second_len, channels
    )
    twist_cos, twist_sin = angle_tables(first_len, second_len, whole_len)
    twist_cos = twist_cos[:, :, None]
    twist_sin = twist_sin[:, :, None]
    real_two = real_one * twist_cos + imag_one * twist_sin
    imag_two = imag_one * twist_cos - real_one * twist_sin
    cos_second, sin_second = angle_tables(second_len, second_len, second_len)
    real_out = jnp.einsum("amc,ml->alc", real_two, cos_second, precision=highest) + jnp.einsum(
        "amc,ml->alc", imag_two, sin_second, precision=highest
    )
    imag_out = jnp.einsum("amc,ml->alc", imag_two, cos_second, precision=highest) - jnp.einsum(
        "amc,ml->alc", real_two, sin_second, precision=highest
    )
    return (real_out, imag_out)


def signal(real_in, imag_in):
    first_len, second_len, channels = real_in.shape
    lower_half = first_len // 2
    whole_len = first_len * second_len
    cos_second, sin_second = angle_tables(second_len, second_len, second_len)
    real_one = jnp.einsum("alc,lm->amc", real_in, cos_second, precision=highest) - jnp.einsum(
        "alc,lm->amc", imag_in, sin_second, precision=highest
    )
    imag_one = jnp.einsum("alc,lm->amc", real_in, sin_second, precision=highest) + jnp.einsum(
        "alc,lm->amc", imag_in, cos_second, precision=highest
    )
    twist_cos, twist_sin = angle_tables(first_len, second_len, whole_len)
    twist_cos = twist_cos[:, :, None]
    twist_sin = twist_sin[:, :, None]
    real_two = real_one * twist_cos - imag_one * twist_sin
    imag_two = real_one * twist_sin + imag_one * twist_cos
    cos_first, sin_first = angle_tables(lower_half, first_len, first_len)
    merged = jnp.dot(
        cos_first, real_two.reshape(first_len, second_len * channels), precision=highest
    ) - jnp.dot(sin_first, imag_two.reshape(first_len, second_len * channels), precision=highest)
    return merged.reshape(lower_half * second_len, channels) / whole_len


def complex_product(left_real, left_imag, right_real, right_imag):
    return (
        left_real * right_real - left_imag * right_imag,
        left_real * right_imag + left_imag * right_real,
    )


def conj_product(left_real, left_imag, right_real, right_imag):
    return (
        left_real * right_real + left_imag * right_imag,
        left_imag * right_real - left_real * right_imag,
    )


def times_bf16(left_array, right_array):
    return (left_array.astype(jnp.float32) * right_array.astype(jnp.float32)).astype(jnp.bfloat16)


def output_grad(cotangent, out_weight, ready):
    weight_rows = lax.all_gather(out_weight, "lo", axis=0, tiled=True)
    token_rows = lax.all_gather(cotangent, "hi", axis=0, tiled=True)
    weight_rows, token_rows, _ = lax.optimization_barrier((weight_rows, token_rows, ready))
    partial_value = lax.dot_general(
        token_rows,
        weight_rows,
        (((1,), (1,)), ((), ())),
        preferred_element_type=jnp.float32,
    ).astype(jnp.bfloat16)
    tp_parts = lax.axis_size("tp")
    chunks = partial_value.reshape((tp_parts, -1) + partial_value.shape[1:])
    received = lax.all_to_all(chunks, "tp", split_axis=0, concat_axis=0, tiled=True)
    summed = jnp.sum(received.astype(jnp.float32), axis=0).astype(jnp.bfloat16)
    hi_count = lax.axis_size("hi")
    tp_count = lax.axis_size("tp")
    pairs = [
        (row * tp_count + col, col * tp_count + row)
        for row in range(hi_count)
        for col in range(tp_count)
    ]
    return lax.ppermute(summed, ("hi", "tp"), pairs)


def butterfly_sum(value, axis):
    devices = lax.axis_size(axis)
    stride = 1
    while stride < devices:
        value = value + lax.ppermute(value, axis, [(i, i ^ stride) for i in range(devices)])
        stride *= 2
    return value


def body(proj, cotangent, out_weight, short_weight, long_filter):
    tok_rows = proj.shape[0]
    channels = proj.shape[2]
    taps_count = short_weight.shape[0]
    rim_rows = taps_count - 1
    lower_rows = shifted(proj[tok_rows - rim_rows :], SEQ, 1)
    extended = jnp.concatenate([lower_rows, proj], axis=0)
    primed = short_weight[0] * extended[rim_rows : rim_rows + tok_rows]
    for offset in range(1, taps_count):
        primed = (
            primed
            + short_weight[offset] * extended[rim_rows - offset : rim_rows - offset + tok_rows]
        )
    primed = primed.astype(jnp.bfloat16)
    query_conv = primed[:, 0]
    keys_conv = primed[:, 1]
    value_conv = primed[:, 2]
    gated_input = times_bf16(keys_conv, value_conv)
    filter_cols = lax.all_to_all(
        long_filter.astype(jnp.bfloat16), SEQ, split_axis=1, concat_axis=0, tiled=True
    ).astype(long_filter.dtype)
    filter_real, filter_imag = spectrum(filter_cols)
    gated_cols = lax.all_to_all(gated_input, SEQ, split_axis=1, concat_axis=0, tiled=True)
    gated_real, gated_imag = spectrum(gated_cols)
    conv_cols = signal(*complex_product(gated_real, gated_imag, filter_real, filter_imag)).astype(
        jnp.bfloat16
    )
    conv_out = lax.all_to_all(conv_cols, SEQ, split_axis=0, concat_axis=1, tiled=True)
    grad_out = output_grad(cotangent, out_weight, conv_out)
    grad_query = times_bf16(grad_out, conv_out)
    grad_conv = times_bf16(grad_out, query_conv)
    grad_cols = lax.all_to_all(grad_conv, SEQ, split_axis=1, concat_axis=0, tiled=True)
    grad_real, grad_imag = spectrum(grad_cols)
    gated_grad_cols = signal(*conj_product(grad_real, grad_imag, filter_real, filter_imag)).astype(
        jnp.bfloat16
    )
    filter_grad_cols = signal(*conj_product(grad_real, grad_imag, gated_real, gated_imag))
    gated_grad = lax.all_to_all(gated_grad_cols, SEQ, split_axis=0, concat_axis=1, tiled=True)
    grad_filter = lax.all_to_all(
        filter_grad_cols.astype(jnp.bfloat16), SEQ, split_axis=0, concat_axis=1, tiled=True
    ).astype(filter_grad_cols.dtype)
    grad_keys = times_bf16(gated_grad, value_conv)
    grad_value = times_bf16(gated_grad, keys_conv)
    grad_primed = jnp.stack([grad_query, grad_keys, grad_value], axis=1)
    next_rows = shifted(grad_primed[:rim_rows], SEQ, -1)
    trailing = jnp.concatenate([grad_primed, next_rows], axis=0)
    grad_sum = short_weight[0] * trailing[0:tok_rows]
    for offset in range(1, taps_count):
        grad_sum = grad_sum + short_weight[offset] * trailing[offset : offset + tok_rows]
    grad_proj = grad_sum.astype(jnp.bfloat16)
    grad_wide = grad_primed.astype(jnp.float32)
    local_short = jnp.stack(
        [
            jnp.sum(
                grad_wide
                * extended[rim_rows - offset : rim_rows - offset + tok_rows].astype(jnp.float32),
                axis=0,
            )
            for offset in range(taps_count)
        ]
    )
    grad_short = butterfly_sum(local_short, SEQ)
    return (grad_proj, grad_short, grad_filter)


def solution(mesh):
    seq_count = mesh.shape["seq"]
    tp_count = mesh.shape["tp"]
    split_mesh = jax.sharding.Mesh(
        mesh.devices.reshape(tp_count, seq_count // tp_count, tp_count), ("hi", "lo", "tp")
    )
    in_specs = (
        P(SEQ, None, "tp"),
        P(SEQ, "tp"),
        P(SEQ, "tp"),
        P(None, None, "tp"),
        P(SEQ, "tp"),
    )
    out_specs = (P(SEQ, None, "tp"), P(None, None, "tp"), P(SEQ, "tp"))
    return jax.shard_map(
        body, mesh=split_mesh, in_specs=in_specs, out_specs=out_specs, check_vma=False
    )
```

```python
import math

import jax
import jax.numpy as jnp
from jax import lax
from jax.sharding import PartitionSpec as P

highest = lax.Precision.DEFAULT
SEQ = ("hi", "lo")


def shifted(value, axis, by):
    devices = lax.axis_size(axis)
    pairs = [(i, i + by) for i in range(devices) if 0 <= i + by < devices]
    return lax.ppermute(value, axis, pairs)


def angle_tables(row_count, col_count, modulus):
    row_index = jnp.arange(row_count, dtype=jnp.int32)[:, None]
    col_index = jnp.arange(col_count, dtype=jnp.int32)[None, :]
    phase = (row_index * col_index % modulus).astype(jnp.float32) * (2.0 * math.pi / modulus)
    return (jnp.cos(phase), jnp.sin(phase))


def split_length(length):
    whole_len = 2 * length
    ceiling = 1 << whole_len.bit_length() // 2 - 1
    first_len = 2 * math.gcd(length, ceiling)
    return (first_len, whole_len // first_len)


def spectrum(columns):
    length, channels = columns.shape
    first_len, second_len = split_length(length)
    lower_half = first_len // 2
    whole_len = first_len * second_len
    values = columns.astype(jnp.float32).reshape(lower_half, second_len * channels)
    cos_first, sin_first = angle_tables(first_len, lower_half, first_len)
    real_one = jnp.dot(cos_first, values, precision=highest).reshape(
        first_len, second_len, channels
    )
    imag_one = -jnp.dot(sin_first, values, precision=highest).reshape(
        first_len, second_len, channels
    )
    twist_cos, twist_sin = angle_tables(first_len, second_len, whole_len)
    twist_cos = twist_cos[:, :, None]
    twist_sin = twist_sin[:, :, None]
    real_two = real_one * twist_cos + imag_one * twist_sin
    imag_two = imag_one * twist_cos - real_one * twist_sin
    cos_second, sin_second = angle_tables(second_len, second_len, second_len)
    real_out = jnp.einsum("amc,ml->alc", real_two, cos_second, precision=highest) + jnp.einsum(
        "amc,ml->alc", imag_two, sin_second, precision=highest
    )
    imag_out = jnp.einsum("amc,ml->alc", imag_two, cos_second, precision=highest) - jnp.einsum(
        "amc,ml->alc", real_two, sin_second, precision=highest
    )
    return (real_out, imag_out)


def signal(real_in, imag_in):
    first_len, second_len, channels = real_in.shape
    lower_half = first_len // 2
    whole_len = first_len * second_len
    cos_second, sin_second = angle_tables(second_len, second_len, second_len)
    real_one = jnp.einsum("alc,lm->amc", real_in, cos_second, precision=highest) - jnp.einsum(
        "alc,lm->amc", imag_in, sin_second, precision=highest
    )
    imag_one = jnp.einsum("alc,lm->amc", real_in, sin_second, precision=highest) + jnp.einsum(
        "alc,lm->amc", imag_in, cos_second, precision=highest
    )
    twist_cos, twist_sin = angle_tables(first_len, second_len, whole_len)
    twist_cos = twist_cos[:, :, None]
    twist_sin = twist_sin[:, :, None]
    real_two = real_one * twist_cos - imag_one * twist_sin
    imag_two = real_one * twist_sin + imag_one * twist_cos
    cos_first, sin_first = angle_tables(lower_half, first_len, first_len)
    merged = jnp.dot(
        cos_first, real_two.reshape(first_len, second_len * channels), precision=highest
    ) - jnp.dot(sin_first, imag_two.reshape(first_len, second_len * channels), precision=highest)
    return merged.reshape(lower_half * second_len, channels) / whole_len


def complex_product(left_real, left_imag, right_real, right_imag):
    return (
        left_real * right_real - left_imag * right_imag,
        left_real * right_imag + left_imag * right_real,
    )


def conj_product(left_real, left_imag, right_real, right_imag):
    return (
        left_real * right_real + left_imag * right_imag,
        left_imag * right_real - left_real * right_imag,
    )


def times_bf16(left_array, right_array):
    return (left_array.astype(jnp.float32) * right_array.astype(jnp.float32)).astype(jnp.bfloat16)


def output_grad(cotangent, out_weight, ready):
    weight_rows = lax.all_gather(out_weight, "lo", axis=0, tiled=True)
    token_rows = lax.all_gather(cotangent, "hi", axis=0, tiled=True)
    weight_rows, token_rows, _ = lax.optimization_barrier((weight_rows, token_rows, ready))
    partial_value = lax.dot_general(
        token_rows,
        weight_rows,
        (((1,), (1,)), ((), ())),
        preferred_element_type=jnp.float32,
    ).astype(jnp.bfloat16)
    tp_parts = lax.axis_size("tp")
    chunks = partial_value.reshape((tp_parts, -1) + partial_value.shape[1:])
    received = lax.all_to_all(chunks, "tp", split_axis=0, concat_axis=0, tiled=True)
    summed = jnp.sum(received.astype(jnp.float32), axis=0).astype(jnp.bfloat16)
    hi_count = lax.axis_size("hi")
    tp_count = lax.axis_size("tp")
    pairs = [
        (row * tp_count + col, col * tp_count + row)
        for row in range(hi_count)
        for col in range(tp_count)
    ]
    return lax.ppermute(summed, ("hi", "tp"), pairs)


def butterfly_sum(value, axis):
    devices = lax.axis_size(axis)
    stride = 1
    while stride < devices:
        value = value + lax.ppermute(value, axis, [(i, i ^ stride) for i in range(devices)])
        stride *= 2
    return value


def body(proj, cotangent, out_weight, short_weight, long_filter):
    tok_rows = proj.shape[0]
    channels = proj.shape[2]
    taps_count = short_weight.shape[0]
    rim_rows = taps_count - 1
    lower_rows = shifted(proj[tok_rows - rim_rows :], SEQ, 1)
    extended = jnp.concatenate([lower_rows, proj], axis=0)
    primed = short_weight[0] * extended[rim_rows : rim_rows + tok_rows]
    for offset in range(1, taps_count):
        primed = (
            primed
            + short_weight[offset] * extended[rim_rows - offset : rim_rows - offset + tok_rows]
        )
    primed = primed.astype(jnp.bfloat16)
    query_conv = primed[:, 0]
    keys_conv = primed[:, 1]
    value_conv = primed[:, 2]
    gated_input = times_bf16(keys_conv, value_conv)
    filter_cols = lax.all_to_all(
        long_filter.astype(jnp.bfloat16), SEQ, split_axis=1, concat_axis=0, tiled=True
    ).astype(long_filter.dtype)
    filter_real, filter_imag = spectrum(filter_cols)
    gated_cols = lax.all_to_all(gated_input, SEQ, split_axis=1, concat_axis=0, tiled=True)
    gated_real, gated_imag = spectrum(gated_cols)
    conv_cols = signal(*complex_product(gated_real, gated_imag, filter_real, filter_imag)).astype(
        jnp.bfloat16
    )
    conv_out = lax.all_to_all(conv_cols, SEQ, split_axis=0, concat_axis=1, tiled=True)
    grad_out = output_grad(cotangent, out_weight, conv_out)
    grad_query = times_bf16(grad_out, conv_out)
    grad_conv = times_bf16(grad_out, query_conv)
    grad_cols = lax.all_to_all(grad_conv, SEQ, split_axis=1, concat_axis=0, tiled=True)
    grad_real, grad_imag = spectrum(grad_cols)
    gated_grad_cols = signal(*conj_product(grad_real, grad_imag, filter_real, filter_imag)).astype(
        jnp.bfloat16
    )
    filter_grad_cols = signal(*conj_product(grad_real, grad_imag, gated_real, gated_imag))
    gated_grad = lax.all_to_all(gated_grad_cols, SEQ, split_axis=0, concat_axis=1, tiled=True)
    grad_filter = lax.all_to_all(
        filter_grad_cols.astype(jnp.bfloat16), SEQ, split_axis=0, concat_axis=1, tiled=True
    ).astype(filter_grad_cols.dtype)
    grad_keys = times_bf16(gated_grad, value_conv)
    grad_value = times_bf16(gated_grad, keys_conv)
    grad_primed = jnp.stack([grad_query, grad_keys, grad_value], axis=1)
    next_rows = shifted(grad_primed[:rim_rows], SEQ, -1)
    trailing = jnp.concatenate([grad_primed, next_rows], axis=0)
    grad_sum = short_weight[0] * trailing[0:tok_rows]
    for offset in range(1, taps_count):
        grad_sum = grad_sum + short_weight[offset] * trailing[offset : offset + tok_rows]
    grad_proj = grad_sum.astype(jnp.bfloat16)
    grad_wide = grad_primed.astype(jnp.float32)
    local_short = jnp.stack(
        [
            jnp.sum(
                grad_wide
                * extended[rim_rows - offset : rim_rows - offset + tok_rows].astype(jnp.float32),
                axis=0,
            )
            for offset in range(taps_count)
        ]
    )
    grad_short = butterfly_sum(local_short, SEQ)
    return (grad_proj, grad_short, grad_filter)


def solution(mesh):
    seq_count = mesh.shape["seq"]
    tp_count = mesh.shape["tp"]
    split_mesh = jax.sharding.Mesh(
        mesh.devices.reshape(tp_count, seq_count // tp_count, tp_count), ("hi", "lo", "tp")
    )
    in_specs = (
        P(SEQ, None, "tp"),
        P(SEQ, "tp"),
        P(SEQ, "tp"),
        P(None, None, "tp"),
        P(SEQ, "tp"),
    )
    out_specs = (P(SEQ, None, "tp"), P(None, None, "tp"), P(SEQ, "tp"))
    return jax.shard_map(
        body, mesh=split_mesh, in_specs=in_specs, out_specs=out_specs, check_vma=False
    )
```

```python
import math

import jax
import jax.numpy as jnp
from jax import lax
from jax.sharding import PartitionSpec as P

highest = lax.Precision.HIGH
SEQ = ("hi", "lo")


def shifted(value, axis, by):
    devices = lax.axis_size(axis)
    pairs = [(i, i + by) for i in range(devices) if 0 <= i + by < devices]
    return lax.ppermute(value, axis, pairs)


def angle_tables(row_count, col_count, modulus):
    row_index = jnp.arange(row_count, dtype=jnp.int32)[:, None]
    col_index = jnp.arange(col_count, dtype=jnp.int32)[None, :]
    phase = (row_index * col_index % modulus).astype(jnp.float32) * (2.0 * math.pi / modulus)
    return (jnp.cos(phase), jnp.sin(phase))


def split_length(length):
    whole_len = 2 * length
    ceiling = 1 << whole_len.bit_length() // 2 - 1
    first_len = 2 * math.gcd(length, ceiling)
    return (first_len, whole_len // first_len)


def spectrum(columns):
    length, channels = columns.shape
    first_len, second_len = split_length(length)
    lower_half = first_len // 2
    whole_len = first_len * second_len
    values = columns.astype(jnp.float32).reshape(lower_half, second_len * channels)
    cos_first, sin_first = angle_tables(first_len, lower_half, first_len)
    real_one = jnp.dot(cos_first, values, precision=highest).reshape(
        first_len, second_len, channels
    )
    imag_one = -jnp.dot(sin_first, values, precision=highest).reshape(
        first_len, second_len, channels
    )
    twist_cos, twist_sin = angle_tables(first_len, second_len, whole_len)
    twist_cos = twist_cos[:, :, None]
    twist_sin = twist_sin[:, :, None]
    real_two = real_one * twist_cos + imag_one * twist_sin
    imag_two = imag_one * twist_cos - real_one * twist_sin
    cos_second, sin_second = angle_tables(second_len, second_len, second_len)
    real_out = jnp.einsum("amc,ml->alc", real_two, cos_second, precision=highest) + jnp.einsum(
        "amc,ml->alc", imag_two, sin_second, precision=highest
    )
    imag_out = jnp.einsum("amc,ml->alc", imag_two, cos_second, precision=highest) - jnp.einsum(
        "amc,ml->alc", real_two, sin_second, precision=highest
    )
    return (real_out, imag_out)


def signal(real_in, imag_in):
    first_len, second_len, channels = real_in.shape
    lower_half = first_len // 2
    whole_len = first_len * second_len
    cos_second, sin_second = angle_tables(second_len, second_len, second_len)
    real_one = jnp.einsum("alc,lm->amc", real_in, cos_second, precision=highest) - jnp.einsum(
        "alc,lm->amc", imag_in, sin_second, precision=highest
    )
    imag_one = jnp.einsum("alc,lm->amc", real_in, sin_second, precision=highest) + jnp.einsum(
        "alc,lm->amc", imag_in, cos_second, precision=highest
    )
    twist_cos, twist_sin = angle_tables(first_len, second_len, whole_len)
    twist_cos = twist_cos[:, :, None]
    twist_sin = twist_sin[:, :, None]
    real_two = real_one * twist_cos - imag_one * twist_sin
    imag_two = real_one * twist_sin + imag_one * twist_cos
    cos_first, sin_first = angle_tables(lower_half, first_len, first_len)
    merged = jnp.dot(
        cos_first, real_two.reshape(first_len, second_len * channels), precision=highest
    ) - jnp.dot(sin_first, imag_two.reshape(first_len, second_len * channels), precision=highest)
    return merged.reshape(lower_half * second_len, channels) / whole_len


def complex_product(left_real, left_imag, right_real, right_imag):
    return (
        left_real * right_real - left_imag * right_imag,
        left_real * right_imag + left_imag * right_real,
    )


def conj_product(left_real, left_imag, right_real, right_imag):
    return (
        left_real * right_real + left_imag * right_imag,
        left_imag * right_real - left_real * right_imag,
    )


def times_bf16(left_array, right_array):
    return (left_array.astype(jnp.float32) * right_array.astype(jnp.float32)).astype(jnp.bfloat16)


SHORT_ROUTES = (
    (0, 6, 1, 4, 3, 5, 2, 7),
    (7, 0, 4, 1, 5, 2, 6, 3),
    (0, 5, 1, 4, 2, 6, 3, 7),
    (4, 0, 5, 1, 6, 2, 7, 3),
    (4, 0, 5, 1, 6, 2, 7, 3),
    (0, 4, 1, 5, 3, 6, 2, 7),
    (4, 1, 5, 2, 6, 3, 7, 0),
    (0, 4, 2, 6, 3, 5, 1, 7),
)


def chunk_orders(hi_count, tp_count):
    if hi_count == len(SHORT_ROUTES) and tp_count == len(SHORT_ROUTES[0]):
        return SHORT_ROUTES
    return tuple(tuple(range(tp_count)) for _ in range(hi_count))


def output_grad(cotangent, out_weight, ready):
    weight_rows = lax.all_gather(out_weight, "lo", axis=0, tiled=True)
    token_rows = lax.all_gather(cotangent, "hi", axis=0, tiled=True)
    weight_rows, token_rows, _ = lax.optimization_barrier((weight_rows, token_rows, ready))
    partial_value = lax.dot_general(
        token_rows,
        weight_rows,
        (((1,), (1,)), ((), ())),
        preferred_element_type=jnp.float32,
    ).astype(jnp.bfloat16)
    tp_parts = lax.axis_size("tp")
    hi_count = lax.axis_size("hi")
    orders = chunk_orders(hi_count, tp_parts)
    order_row = jnp.asarray(orders, jnp.int32)[lax.axis_index("hi")]
    chunks = partial_value.reshape((tp_parts, -1) + partial_value.shape[1:])[order_row]
    received = lax.all_to_all(chunks, "tp", split_axis=0, concat_axis=0, tiled=True)
    summed = jnp.sum(received.astype(jnp.float32), axis=0).astype(jnp.bfloat16)
    pairs = [
        (row * tp_parts + col, orders[row][col] * tp_parts + row)
        for row in range(hi_count)
        for col in range(tp_parts)
    ]
    return lax.ppermute(summed, ("hi", "tp"), pairs)


def butterfly_sum(value, axis):
    devices = lax.axis_size(axis)
    stride = 1
    while stride < devices:
        value = value + lax.ppermute(value, axis, [(i, i ^ stride) for i in range(devices)])
        stride *= 2
    return value


def body(proj, cotangent, out_weight, short_weight, long_filter):
    tok_rows = proj.shape[0]
    channels = proj.shape[2]
    taps_count = short_weight.shape[0]
    rim_rows = taps_count - 1
    lower_rows = shifted(proj[tok_rows - rim_rows :], SEQ, 1)
    extended = jnp.concatenate([lower_rows, proj], axis=0)
    primed = short_weight[0] * extended[rim_rows : rim_rows + tok_rows]
    for offset in range(1, taps_count):
        primed = (
            primed
            + short_weight[offset] * extended[rim_rows - offset : rim_rows - offset + tok_rows]
        )
    primed = primed.astype(jnp.bfloat16)
    query_conv = primed[:, 0]
    keys_conv = primed[:, 1]
    value_conv = primed[:, 2]
    gated_input = times_bf16(keys_conv, value_conv)
    filter_cols = lax.all_to_all(
        long_filter.astype(jnp.bfloat16), SEQ, split_axis=1, concat_axis=0, tiled=True
    ).astype(long_filter.dtype)
    filter_real, filter_imag = spectrum(filter_cols)
    gated_cols = lax.all_to_all(gated_input, SEQ, split_axis=1, concat_axis=0, tiled=True)
    gated_real, gated_imag = spectrum(gated_cols)
    conv_cols = signal(*complex_product(gated_real, gated_imag, filter_real, filter_imag)).astype(
        jnp.bfloat16
    )
    conv_out = lax.all_to_all(conv_cols, SEQ, split_axis=0, concat_axis=1, tiled=True)
    grad_out = output_grad(cotangent, out_weight, conv_out)
    grad_query = times_bf16(grad_out, conv_out)
    grad_conv = times_bf16(grad_out, query_conv)
    grad_cols = lax.all_to_all(grad_conv, SEQ, split_axis=1, concat_axis=0, tiled=True)
    grad_real, grad_imag = spectrum(grad_cols)
    gated_grad_cols = signal(*conj_product(grad_real, grad_imag, filter_real, filter_imag)).astype(
        jnp.bfloat16
    )
    filter_grad_cols = signal(*conj_product(grad_real, grad_imag, gated_real, gated_imag))
    gated_grad = lax.all_to_all(gated_grad_cols, SEQ, split_axis=0, concat_axis=1, tiled=True)
    grad_filter = lax.all_to_all(
        filter_grad_cols.astype(jnp.bfloat16), SEQ, split_axis=0, concat_axis=1, tiled=True
    ).astype(filter_grad_cols.dtype)
    grad_keys = times_bf16(gated_grad, value_conv)
    grad_value = times_bf16(gated_grad, keys_conv)
    grad_primed = jnp.stack([grad_query, grad_keys, grad_value], axis=1)
    next_rows = shifted(grad_primed[:rim_rows], SEQ, -1)
    trailing = jnp.concatenate([grad_primed, next_rows], axis=0)
    grad_sum = short_weight[0] * trailing[0:tok_rows]
    for offset in range(1, taps_count):
        grad_sum = grad_sum + short_weight[offset] * trailing[offset : offset + tok_rows]
    grad_proj = grad_sum.astype(jnp.bfloat16)
    grad_wide = grad_primed.astype(jnp.float32)
    local_short = jnp.stack(
        [
            jnp.sum(
                grad_wide
                * extended[rim_rows - offset : rim_rows - offset + tok_rows].astype(jnp.float32),
                axis=0,
            )
            for offset in range(taps_count)
        ]
    )
    grad_short = butterfly_sum(local_short, SEQ)
    return (grad_proj, grad_short, grad_filter)


def solution(mesh):
    seq_count = mesh.shape["seq"]
    tp_count = mesh.shape["tp"]
    split_mesh = jax.sharding.Mesh(
        mesh.devices.reshape(tp_count, seq_count // tp_count, tp_count), ("hi", "lo", "tp")
    )
    in_specs = (
        P(SEQ, None, "tp"),
        P(SEQ, "tp"),
        P(SEQ, "tp"),
        P(None, None, "tp"),
        P(SEQ, "tp"),
    )
    out_specs = (P(SEQ, None, "tp"), P(None, None, "tp"), P(SEQ, "tp"))
    return jax.shard_map(
        body, mesh=split_mesh, in_specs=in_specs, out_specs=out_specs, check_vma=False
    )
```

```python
import math

import jax
import jax.numpy as jnp
from jax import lax
from jax.sharding import PartitionSpec as P

highest = lax.Precision.HIGH
SEQ = ("hi", "lo")


def shifted(value, axis, by):
    devices = lax.axis_size(axis)
    pairs = [(i, i + by) for i in range(devices) if 0 <= i + by < devices]
    return lax.ppermute(value, axis, pairs)


def angle_tables(row_count, col_count, modulus):
    row_index = jnp.arange(row_count, dtype=jnp.int32)[:, None]
    col_index = jnp.arange(col_count, dtype=jnp.int32)[None, :]
    phase = (row_index * col_index % modulus).astype(jnp.float32) * (2.0 * math.pi / modulus)
    return (jnp.cos(phase), jnp.sin(phase))


def split_length(length):
    whole_len = 2 * length
    ceiling = 1 << whole_len.bit_length() // 2 - 1
    first_len = 2 * math.gcd(length, ceiling)
    return (first_len, whole_len // first_len)


def spectrum(columns):
    length, channels = columns.shape
    first_len, second_len = split_length(length)
    lower_half = first_len // 2
    whole_len = first_len * second_len
    values = columns.astype(jnp.float32).reshape(lower_half, second_len * channels)
    cos_first, sin_first = angle_tables(first_len, lower_half, first_len)
    real_one = jnp.dot(cos_first, values, precision=highest).reshape(
        first_len, second_len, channels
    )
    imag_one = -jnp.dot(sin_first, values, precision=highest).reshape(
        first_len, second_len, channels
    )
    twist_cos, twist_sin = angle_tables(first_len, second_len, whole_len)
    twist_cos = twist_cos[:, :, None]
    twist_sin = twist_sin[:, :, None]
    real_two = real_one * twist_cos + imag_one * twist_sin
    imag_two = imag_one * twist_cos - real_one * twist_sin
    cos_second, sin_second = angle_tables(second_len, second_len, second_len)
    real_out = jnp.einsum("amc,ml->alc", real_two, cos_second, precision=highest) + jnp.einsum(
        "amc,ml->alc", imag_two, sin_second, precision=highest
    )
    imag_out = jnp.einsum("amc,ml->alc", imag_two, cos_second, precision=highest) - jnp.einsum(
        "amc,ml->alc", real_two, sin_second, precision=highest
    )
    return (real_out, imag_out)


def signal(real_in, imag_in):
    first_len, second_len, channels = real_in.shape
    lower_half = first_len // 2
    whole_len = first_len * second_len
    cos_second, sin_second = angle_tables(second_len, second_len, second_len)
    real_one = jnp.einsum("alc,lm->amc", real_in, cos_second, precision=highest) - jnp.einsum(
        "alc,lm->amc", imag_in, sin_second, precision=highest
    )
    imag_one = jnp.einsum("alc,lm->amc", real_in, sin_second, precision=highest) + jnp.einsum(
        "alc,lm->amc", imag_in, cos_second, precision=highest
    )
    twist_cos, twist_sin = angle_tables(first_len, second_len, whole_len)
    twist_cos = twist_cos[:, :, None]
    twist_sin = twist_sin[:, :, None]
    real_two = real_one * twist_cos - imag_one * twist_sin
    imag_two = real_one * twist_sin + imag_one * twist_cos
    cos_first, sin_first = angle_tables(lower_half, first_len, first_len)
    merged = jnp.dot(
        cos_first, real_two.reshape(first_len, second_len * channels), precision=highest
    ) - jnp.dot(sin_first, imag_two.reshape(first_len, second_len * channels), precision=highest)
    return merged.reshape(lower_half * second_len, channels) / whole_len


def complex_product(left_real, left_imag, right_real, right_imag):
    return (
        left_real * right_real - left_imag * right_imag,
        left_real * right_imag + left_imag * right_real,
    )


def conj_product(left_real, left_imag, right_real, right_imag):
    return (
        left_real * right_real + left_imag * right_imag,
        left_imag * right_real - left_real * right_imag,
    )


def times_bf16(left_array, right_array):
    return (left_array.astype(jnp.float32) * right_array.astype(jnp.float32)).astype(jnp.bfloat16)


def reduced_block(token_rows, weight_rows):
    partial_value = lax.dot_general(
        token_rows,
        weight_rows,
        (((1,), (1,)), ((), ())),
        preferred_element_type=jnp.float32,
    ).astype(jnp.bfloat16)
    tp_parts = lax.axis_size("tp")
    chunks = partial_value.reshape((tp_parts, -1) + partial_value.shape[1:])
    received = lax.all_to_all(chunks, "tp", split_axis=0, concat_axis=0, tiled=True)
    return jnp.sum(received.astype(jnp.float32), axis=0).astype(jnp.bfloat16)


def output_grad(cotangent, out_weight, ready):
    half = cotangent.shape[0] // 2
    weight_rows = lax.all_gather(out_weight, "lo", axis=0, tiled=True)
    first_rows = lax.all_gather(cotangent[:half], "hi", axis=0, tiled=True)
    second_rows = lax.all_gather(cotangent[half:], "hi", axis=0, tiled=True)
    weight_rows, first_rows, ready = lax.optimization_barrier((weight_rows, first_rows, ready))
    first_sum = reduced_block(first_rows, weight_rows)
    second_rows, first_sum = lax.optimization_barrier((second_rows, first_sum))
    second_sum = reduced_block(second_rows, weight_rows)
    summed = jnp.concatenate([first_sum, second_sum], axis=0)
    hi_count = lax.axis_size("hi")
    tp_count = lax.axis_size("tp")
    pairs = [
        (row * tp_count + col, col * tp_count + row)
        for row in range(hi_count)
        for col in range(tp_count)
    ]
    return lax.ppermute(summed, ("hi", "tp"), pairs), ready


def butterfly_sum(value, axis):
    devices = lax.axis_size(axis)
    stride = 1
    while stride < devices:
        value = value + lax.ppermute(value, axis, [(i, i ^ stride) for i in range(devices)])
        stride *= 2
    return value


def body(proj, cotangent, out_weight, short_weight, long_filter):
    tok_rows = proj.shape[0]
    channels = proj.shape[2]
    taps_count = short_weight.shape[0]
    rim_rows = taps_count - 1
    lower_rows = shifted(proj[tok_rows - rim_rows :], SEQ, 1)
    extended = jnp.concatenate([lower_rows, proj], axis=0)
    primed = short_weight[0] * extended[rim_rows : rim_rows + tok_rows]
    for offset in range(1, taps_count):
        primed = (
            primed
            + short_weight[offset] * extended[rim_rows - offset : rim_rows - offset + tok_rows]
        )
    primed = primed.astype(jnp.bfloat16)
    query_conv = primed[:, 0]
    keys_conv = primed[:, 1]
    value_conv = primed[:, 2]
    gated_input = times_bf16(keys_conv, value_conv)
    filter_cols = lax.all_to_all(
        long_filter.astype(jnp.bfloat16), SEQ, split_axis=1, concat_axis=0, tiled=True
    ).astype(long_filter.dtype)
    filter_real, filter_imag = spectrum(filter_cols)
    gated_cols = lax.all_to_all(gated_input, SEQ, split_axis=1, concat_axis=0, tiled=True)
    gated_real, gated_imag = spectrum(gated_cols)
    conv_cols = signal(*complex_product(gated_real, gated_imag, filter_real, filter_imag)).astype(
        jnp.bfloat16
    )
    conv_out = lax.all_to_all(conv_cols, SEQ, split_axis=0, concat_axis=1, tiled=True)
    grad_out, conv_out = output_grad(cotangent, out_weight, conv_out)
    grad_query = times_bf16(grad_out, conv_out)
    grad_conv = times_bf16(grad_out, query_conv)
    grad_cols = lax.all_to_all(grad_conv, SEQ, split_axis=1, concat_axis=0, tiled=True)
    grad_real, grad_imag = spectrum(grad_cols)
    gated_grad_cols = signal(*conj_product(grad_real, grad_imag, filter_real, filter_imag)).astype(
        jnp.bfloat16
    )
    filter_grad_cols = signal(*conj_product(grad_real, grad_imag, gated_real, gated_imag))
    gated_grad = lax.all_to_all(gated_grad_cols, SEQ, split_axis=0, concat_axis=1, tiled=True)
    grad_filter = lax.all_to_all(
        filter_grad_cols.astype(jnp.bfloat16), SEQ, split_axis=0, concat_axis=1, tiled=True
    ).astype(filter_grad_cols.dtype)
    grad_keys = times_bf16(gated_grad, value_conv)
    grad_value = times_bf16(gated_grad, keys_conv)
    grad_primed = jnp.stack([grad_query, grad_keys, grad_value], axis=1)
    next_rows = shifted(grad_primed[:rim_rows], SEQ, -1)
    trailing = jnp.concatenate([grad_primed, next_rows], axis=0)
    grad_sum = short_weight[0] * trailing[0:tok_rows]
    for offset in range(1, taps_count):
        grad_sum = grad_sum + short_weight[offset] * trailing[offset : offset + tok_rows]
    grad_proj = grad_sum.astype(jnp.bfloat16)
    grad_wide = grad_primed.astype(jnp.float32)
    local_short = jnp.stack(
        [
            jnp.sum(
                grad_wide
                * extended[rim_rows - offset : rim_rows - offset + tok_rows].astype(jnp.float32),
                axis=0,
            )
            for offset in range(taps_count)
        ]
    )
    grad_short = butterfly_sum(local_short, SEQ)
    return (grad_proj, grad_short, grad_filter)


def solution(mesh):
    seq_count = mesh.shape["seq"]
    tp_count = mesh.shape["tp"]
    split_mesh = jax.sharding.Mesh(
        mesh.devices.reshape(tp_count, seq_count // tp_count, tp_count), ("hi", "lo", "tp")
    )
    in_specs = (
        P(SEQ, None, "tp"),
        P(SEQ, "tp"),
        P(SEQ, "tp"),
        P(None, None, "tp"),
        P(SEQ, "tp"),
    )
    out_specs = (P(SEQ, None, "tp"), P(None, None, "tp"), P(SEQ, "tp"))
    return jax.shard_map(
        body, mesh=split_mesh, in_specs=in_specs, out_specs=out_specs, check_vma=False
    )
```

```python
import math

import jax
import jax.numpy as jnp
from jax import lax
from jax.sharding import PartitionSpec as P

highest = lax.Precision.DEFAULT
SEQ = ("hi", "lo")


def shifted(value, axis, by):
    devices = lax.axis_size(axis)
    pairs = [(i, i + by) for i in range(devices) if 0 <= i + by < devices]
    return lax.ppermute(value, axis, pairs)


def angle_tables(row_count, col_count, modulus):
    row_index = jnp.arange(row_count, dtype=jnp.int32)[:, None]
    col_index = jnp.arange(col_count, dtype=jnp.int32)[None, :]
    phase = (row_index * col_index % modulus).astype(jnp.float32) * (2.0 * math.pi / modulus)
    return (jnp.cos(phase), jnp.sin(phase))


def split_length(length):
    whole_len = 2 * length
    ceiling = 1 << whole_len.bit_length() // 2 - 1
    first_len = 2 * math.gcd(length, ceiling)
    return (first_len, whole_len // first_len)


def spectrum(columns):
    length, channels = columns.shape
    first_len, second_len = split_length(length)
    lower_half = first_len // 2
    whole_len = first_len * second_len
    values = columns.astype(jnp.float32).reshape(lower_half, second_len * channels)
    cos_first, sin_first = angle_tables(first_len, lower_half, first_len)
    real_one = jnp.dot(cos_first, values, precision=highest).reshape(
        first_len, second_len, channels
    )
    imag_one = -jnp.dot(sin_first, values, precision=highest).reshape(
        first_len, second_len, channels
    )
    twist_cos, twist_sin = angle_tables(first_len, second_len, whole_len)
    twist_cos = twist_cos[:, :, None]
    twist_sin = twist_sin[:, :, None]
    real_two = real_one * twist_cos + imag_one * twist_sin
    imag_two = imag_one * twist_cos - real_one * twist_sin
    cos_second, sin_second = angle_tables(second_len, second_len, second_len)
    real_out = jnp.einsum("amc,ml->alc", real_two, cos_second, precision=highest) + jnp.einsum(
        "amc,ml->alc", imag_two, sin_second, precision=highest
    )
    imag_out = jnp.einsum("amc,ml->alc", imag_two, cos_second, precision=highest) - jnp.einsum(
        "amc,ml->alc", real_two, sin_second, precision=highest
    )
    return (real_out, imag_out)


def signal(real_in, imag_in):
    first_len, second_len, channels = real_in.shape
    lower_half = first_len // 2
    whole_len = first_len * second_len
    cos_second, sin_second = angle_tables(second_len, second_len, second_len)
    real_one = jnp.einsum("alc,lm->amc", real_in, cos_second, precision=highest) - jnp.einsum(
        "alc,lm->amc", imag_in, sin_second, precision=highest
    )
    imag_one = jnp.einsum("alc,lm->amc", real_in, sin_second, precision=highest) + jnp.einsum(
        "alc,lm->amc", imag_in, cos_second, precision=highest
    )
    twist_cos, twist_sin = angle_tables(first_len, second_len, whole_len)
    twist_cos = twist_cos[:, :, None]
    twist_sin = twist_sin[:, :, None]
    real_two = real_one * twist_cos - imag_one * twist_sin
    imag_two = real_one * twist_sin + imag_one * twist_cos
    cos_first, sin_first = angle_tables(lower_half, first_len, first_len)
    merged = jnp.dot(
        cos_first, real_two.reshape(first_len, second_len * channels), precision=highest
    ) - jnp.dot(sin_first, imag_two.reshape(first_len, second_len * channels), precision=highest)
    return merged.reshape(lower_half * second_len, channels) / whole_len


def complex_product(left_real, left_imag, right_real, right_imag):
    return (
        left_real * right_real - left_imag * right_imag,
        left_real * right_imag + left_imag * right_real,
    )


def conj_product(left_real, left_imag, right_real, right_imag):
    return (
        left_real * right_real + left_imag * right_imag,
        left_imag * right_real - left_real * right_imag,
    )


def times_bf16(left_array, right_array):
    return (left_array.astype(jnp.float32) * right_array.astype(jnp.float32)).astype(jnp.bfloat16)


def gather_by_all_to_all(value, axis):
    devices = lax.axis_size(axis)
    copies = jnp.broadcast_to(value[None], (devices,) + value.shape)
    gathered = lax.all_to_all(copies, axis, split_axis=0, concat_axis=0, tiled=True)
    return gathered.reshape((-1,) + value.shape[1:])


def output_grad(cotangent, out_weight, ready):
    weight_rows = gather_by_all_to_all(out_weight, "lo")
    token_rows = lax.all_gather(cotangent, "hi", axis=0, tiled=True)
    weight_rows, token_rows, _ = lax.optimization_barrier((weight_rows, token_rows, ready))
    partial_value = lax.dot_general(
        token_rows,
        weight_rows,
        (((1,), (1,)), ((), ())),
        preferred_element_type=jnp.float32,
    ).astype(jnp.bfloat16)
    tp_parts = lax.axis_size("tp")
    chunks = partial_value.reshape((tp_parts, -1) + partial_value.shape[1:])
    received = lax.all_to_all(chunks, "tp", split_axis=0, concat_axis=0, tiled=True)
    summed = jnp.sum(received.astype(jnp.float32), axis=0).astype(jnp.bfloat16)
    hi_count = lax.axis_size("hi")
    tp_count = lax.axis_size("tp")
    pairs = [
        (row * tp_count + col, col * tp_count + row)
        for row in range(hi_count)
        for col in range(tp_count)
    ]
    return lax.ppermute(summed, ("hi", "tp"), pairs)


def butterfly_sum(value, axis):
    devices = lax.axis_size(axis)
    stride = 1
    while stride < devices:
        value = value + lax.ppermute(value, axis, [(i, i ^ stride) for i in range(devices)])
        stride *= 2
    return value


def body(proj, cotangent, out_weight, short_weight, long_filter):
    tok_rows = proj.shape[0]
    channels = proj.shape[2]
    taps_count = short_weight.shape[0]
    rim_rows = taps_count - 1
    lower_rows = shifted(proj[tok_rows - rim_rows :], SEQ, 1)
    extended = jnp.concatenate([lower_rows, proj], axis=0)
    primed = short_weight[0] * extended[rim_rows : rim_rows + tok_rows]
    for offset in range(1, taps_count):
        primed = (
            primed
            + short_weight[offset] * extended[rim_rows - offset : rim_rows - offset + tok_rows]
        )
    primed = primed.astype(jnp.bfloat16)
    query_conv = primed[:, 0]
    keys_conv = primed[:, 1]
    value_conv = primed[:, 2]
    gated_input = times_bf16(keys_conv, value_conv)
    filter_cols = lax.all_to_all(
        long_filter.astype(jnp.bfloat16), SEQ, split_axis=1, concat_axis=0, tiled=True
    ).astype(long_filter.dtype)
    filter_real, filter_imag = spectrum(filter_cols)
    gated_cols = lax.all_to_all(gated_input, SEQ, split_axis=1, concat_axis=0, tiled=True)
    gated_real, gated_imag = spectrum(gated_cols)
    conv_cols = signal(*complex_product(gated_real, gated_imag, filter_real, filter_imag)).astype(
        jnp.bfloat16
    )
    conv_out = lax.all_to_all(conv_cols, SEQ, split_axis=0, concat_axis=1, tiled=True)
    grad_out = output_grad(cotangent, out_weight, conv_out)
    grad_query = times_bf16(grad_out, conv_out)
    grad_conv = times_bf16(grad_out, query_conv)
    grad_cols = lax.all_to_all(grad_conv, SEQ, split_axis=1, concat_axis=0, tiled=True)
    grad_real, grad_imag = spectrum(grad_cols)
    gated_grad_cols = signal(*conj_product(grad_real, grad_imag, filter_real, filter_imag)).astype(
        jnp.bfloat16
    )
    filter_grad_cols = signal(*conj_product(grad_real, grad_imag, gated_real, gated_imag))
    gated_grad = lax.all_to_all(gated_grad_cols, SEQ, split_axis=0, concat_axis=1, tiled=True)
    grad_filter = lax.all_to_all(
        filter_grad_cols.astype(jnp.bfloat16), SEQ, split_axis=0, concat_axis=1, tiled=True
    ).astype(filter_grad_cols.dtype)
    grad_keys = times_bf16(gated_grad, value_conv)
    grad_value = times_bf16(gated_grad, keys_conv)
    grad_primed = jnp.stack([grad_query, grad_keys, grad_value], axis=1)
    next_rows = shifted(grad_primed[:rim_rows], SEQ, -1)
    trailing = jnp.concatenate([grad_primed, next_rows], axis=0)
    grad_sum = short_weight[0] * trailing[0:tok_rows]
    for offset in range(1, taps_count):
        grad_sum = grad_sum + short_weight[offset] * trailing[offset : offset + tok_rows]
    grad_proj = grad_sum.astype(jnp.bfloat16)
    grad_wide = grad_primed.astype(jnp.float32)
    local_short = jnp.stack(
        [
            jnp.sum(
                grad_wide
                * extended[rim_rows - offset : rim_rows - offset + tok_rows].astype(jnp.float32),
                axis=0,
            )
            for offset in range(taps_count)
        ]
    )
    grad_short = butterfly_sum(local_short, SEQ)
    return (grad_proj, grad_short, grad_filter)


def solution(mesh):
    seq_count = mesh.shape["seq"]
    tp_count = mesh.shape["tp"]
    split_mesh = jax.sharding.Mesh(
        mesh.devices.reshape(tp_count, seq_count // tp_count, tp_count), ("hi", "lo", "tp")
    )
    in_specs = (
        P(SEQ, None, "tp"),
        P(SEQ, "tp"),
        P(SEQ, "tp"),
        P(None, None, "tp"),
        P(SEQ, "tp"),
    )
    out_specs = (P(SEQ, None, "tp"), P(None, None, "tp"), P(SEQ, "tp"))
    return jax.shard_map(
        body, mesh=split_mesh, in_specs=in_specs, out_specs=out_specs, check_vma=False
    )
```

```python
import math

import jax
import jax.numpy as jnp
from jax import lax
from jax.sharding import PartitionSpec as P

highest = lax.Precision.DEFAULT
SEQ = ("hi", "lo")


def shifted(value, axis, by):
    devices = lax.axis_size(axis)
    pairs = [(i, i + by) for i in range(devices) if 0 <= i + by < devices]
    return lax.ppermute(value, axis, pairs)


def angle_tables(row_count, col_count, modulus):
    row_index = jnp.arange(row_count, dtype=jnp.int32)[:, None]
    col_index = jnp.arange(col_count, dtype=jnp.int32)[None, :]
    phase = (row_index * col_index % modulus).astype(jnp.float32) * (2.0 * math.pi / modulus)
    return (jnp.cos(phase), jnp.sin(phase))


def split_length(length):
    whole_len = 2 * length
    ceiling = 1 << whole_len.bit_length() // 2 - 1
    first_len = 2 * math.gcd(length, ceiling)
    return (first_len, whole_len // first_len)


def spectrum(columns):
    length, channels = columns.shape
    first_len, second_len = split_length(length)
    lower_half = first_len // 2
    whole_len = first_len * second_len
    values = columns.astype(jnp.float32).reshape(lower_half, second_len * channels)
    cos_first, sin_first = angle_tables(first_len, lower_half, first_len)
    real_one = jnp.dot(cos_first, values, precision=highest).reshape(
        first_len, second_len, channels
    )
    imag_one = -jnp.dot(sin_first, values, precision=highest).reshape(
        first_len, second_len, channels
    )
    twist_cos, twist_sin = angle_tables(first_len, second_len, whole_len)
    twist_cos = twist_cos[:, :, None]
    twist_sin = twist_sin[:, :, None]
    real_two = real_one * twist_cos + imag_one * twist_sin
    imag_two = imag_one * twist_cos - real_one * twist_sin
    cos_second, sin_second = angle_tables(second_len, second_len, second_len)
    real_out = jnp.einsum("amc,ml->alc", real_two, cos_second, precision=highest) + jnp.einsum(
        "amc,ml->alc", imag_two, sin_second, precision=highest
    )
    imag_out = jnp.einsum("amc,ml->alc", imag_two, cos_second, precision=highest) - jnp.einsum(
        "amc,ml->alc", real_two, sin_second, precision=highest
    )
    return (real_out, imag_out)


def signal(real_in, imag_in):
    first_len, second_len, channels = real_in.shape
    lower_half = first_len // 2
    whole_len = first_len * second_len
    cos_second, sin_second = angle_tables(second_len, second_len, second_len)
    real_one = jnp.einsum("alc,lm->amc", real_in, cos_second, precision=highest) - jnp.einsum(
        "alc,lm->amc", imag_in, sin_second, precision=highest
    )
    imag_one = jnp.einsum("alc,lm->amc", real_in, sin_second, precision=highest) + jnp.einsum(
        "alc,lm->amc", imag_in, cos_second, precision=highest
    )
    twist_cos, twist_sin = angle_tables(first_len, second_len, whole_len)
    twist_cos = twist_cos[:, :, None]
    twist_sin = twist_sin[:, :, None]
    real_two = real_one * twist_cos - imag_one * twist_sin
    imag_two = real_one * twist_sin + imag_one * twist_cos
    cos_first, sin_first = angle_tables(lower_half, first_len, first_len)
    merged = jnp.dot(
        cos_first, real_two.reshape(first_len, second_len * channels), precision=highest
    ) - jnp.dot(sin_first, imag_two.reshape(first_len, second_len * channels), precision=highest)
    return merged.reshape(lower_half * second_len, channels) / whole_len


def complex_product(left_real, left_imag, right_real, right_imag):
    return (
        left_real * right_real - left_imag * right_imag,
        left_real * right_imag + left_imag * right_real,
    )


def conj_product(left_real, left_imag, right_real, right_imag):
    return (
        left_real * right_real + left_imag * right_imag,
        left_imag * right_real - left_real * right_imag,
    )


def times_bf16(left_array, right_array):
    return (left_array.astype(jnp.float32) * right_array.astype(jnp.float32)).astype(jnp.bfloat16)


def output_grad(cotangent, out_weight, ready):
    weight_rows = lax.all_gather(out_weight, "lo", axis=0, tiled=True)
    token_rows = lax.all_gather(cotangent, "hi", axis=0, tiled=True)
    weight_rows, token_rows, _ = lax.optimization_barrier((weight_rows, token_rows, ready))
    partial_value = lax.dot_general(
        token_rows,
        weight_rows,
        (((1,), (1,)), ((), ())),
        preferred_element_type=jnp.float32,
    ).astype(jnp.bfloat16)
    tp_parts = lax.axis_size("tp")
    chunks = partial_value.reshape((tp_parts, -1) + partial_value.shape[1:])
    received = lax.all_to_all(chunks, "tp", split_axis=0, concat_axis=0, tiled=True)
    summed = jnp.sum(received.astype(jnp.float32), axis=0).astype(jnp.bfloat16)
    hi_count = lax.axis_size("hi")
    tp_count = lax.axis_size("tp")
    pairs = [
        (row * tp_count + col, col * tp_count + row)
        for row in range(hi_count)
        for col in range(tp_count)
    ]
    return lax.ppermute(summed, ("hi", "tp"), pairs)


def butterfly_sum(value, axis):
    devices = lax.axis_size(axis)
    stride = 1
    while stride < devices:
        sent = value.astype(jnp.bfloat16)
        value = sent.astype(jnp.float32) + lax.ppermute(
            sent, axis, [(i, i ^ stride) for i in range(devices)]
        ).astype(jnp.float32)
        stride *= 2
    return value


def body(proj, cotangent, out_weight, short_weight, long_filter):
    tok_rows = proj.shape[0]
    channels = proj.shape[2]
    taps_count = short_weight.shape[0]
    rim_rows = taps_count - 1
    lower_rows = shifted(proj[tok_rows - rim_rows :], SEQ, 1)
    extended = jnp.concatenate([lower_rows, proj], axis=0)
    primed = short_weight[0] * extended[rim_rows : rim_rows + tok_rows]
    for offset in range(1, taps_count):
        primed = (
            primed
            + short_weight[offset] * extended[rim_rows - offset : rim_rows - offset + tok_rows]
        )
    primed = primed.astype(jnp.bfloat16)
    query_conv = primed[:, 0]
    keys_conv = primed[:, 1]
    value_conv = primed[:, 2]
    gated_input = times_bf16(keys_conv, value_conv)
    filter_cols = lax.all_to_all(
        long_filter.astype(jnp.bfloat16), SEQ, split_axis=1, concat_axis=0, tiled=True
    ).astype(long_filter.dtype)
    filter_real, filter_imag = spectrum(filter_cols)
    gated_cols = lax.all_to_all(gated_input, SEQ, split_axis=1, concat_axis=0, tiled=True)
    gated_real, gated_imag = spectrum(gated_cols)
    conv_cols = signal(*complex_product(gated_real, gated_imag, filter_real, filter_imag)).astype(
        jnp.bfloat16
    )
    conv_out = lax.all_to_all(conv_cols, SEQ, split_axis=0, concat_axis=1, tiled=True)
    grad_out = output_grad(cotangent, out_weight, conv_out)
    grad_query = times_bf16(grad_out, conv_out)
    grad_conv = times_bf16(grad_out, query_conv)
    grad_cols = lax.all_to_all(grad_conv, SEQ, split_axis=1, concat_axis=0, tiled=True)
    grad_real, grad_imag = spectrum(grad_cols)
    gated_grad_cols = signal(*conj_product(grad_real, grad_imag, filter_real, filter_imag)).astype(
        jnp.bfloat16
    )
    filter_grad_cols = signal(*conj_product(grad_real, grad_imag, gated_real, gated_imag))
    gated_grad = lax.all_to_all(gated_grad_cols, SEQ, split_axis=0, concat_axis=1, tiled=True)
    grad_filter = lax.all_to_all(
        filter_grad_cols.astype(jnp.bfloat16), SEQ, split_axis=0, concat_axis=1, tiled=True
    ).astype(filter_grad_cols.dtype)
    grad_keys = times_bf16(gated_grad, value_conv)
    grad_value = times_bf16(gated_grad, keys_conv)
    grad_primed = jnp.stack([grad_query, grad_keys, grad_value], axis=1)
    next_rows = shifted(grad_primed[:rim_rows], SEQ, -1)
    trailing = jnp.concatenate([grad_primed, next_rows], axis=0)
    grad_sum = short_weight[0] * trailing[0:tok_rows]
    for offset in range(1, taps_count):
        grad_sum = grad_sum + short_weight[offset] * trailing[offset : offset + tok_rows]
    grad_proj = grad_sum.astype(jnp.bfloat16)
    grad_wide = grad_primed.astype(jnp.float32)
    local_short = jnp.stack(
        [
            jnp.sum(
                grad_wide
                * extended[rim_rows - offset : rim_rows - offset + tok_rows].astype(jnp.float32),
                axis=0,
            )
            for offset in range(taps_count)
        ]
    )
    grad_short = butterfly_sum(local_short, SEQ)
    return (grad_proj, grad_short, grad_filter)


def solution(mesh):
    seq_count = mesh.shape["seq"]
    tp_count = mesh.shape["tp"]
    split_mesh = jax.sharding.Mesh(
        mesh.devices.reshape(tp_count, seq_count // tp_count, tp_count), ("hi", "lo", "tp")
    )
    in_specs = (
        P(SEQ, None, "tp"),
        P(SEQ, "tp"),
        P(SEQ, "tp"),
        P(None, None, "tp"),
        P(SEQ, "tp"),
    )
    out_specs = (P(SEQ, None, "tp"), P(None, None, "tp"), P(SEQ, "tp"))
    return jax.shard_map(
        body, mesh=split_mesh, in_specs=in_specs, out_specs=out_specs, check_vma=False
    )
```

```python
import math

import jax
import jax.numpy as jnp
from jax import lax
from jax.sharding import PartitionSpec as P

highest = lax.Precision.DEFAULT
SEQ = ("hi", "lo")


def shifted(value, axis, by):
    devices = lax.axis_size(axis)
    pairs = [(i, i + by) for i in range(devices) if 0 <= i + by < devices]
    return lax.ppermute(value, axis, pairs)


def angle_tables(row_count, col_count, modulus):
    row_index = jnp.arange(row_count, dtype=jnp.int32)[:, None]
    col_index = jnp.arange(col_count, dtype=jnp.int32)[None, :]
    phase = (row_index * col_index % modulus).astype(jnp.float32) * (2.0 * math.pi / modulus)
    return (jnp.cos(phase), jnp.sin(phase))


def split_length(length):
    whole_len = 2 * length
    ceiling = 1 << whole_len.bit_length() // 2 - 1
    first_len = 2 * math.gcd(length, ceiling)
    return (first_len, whole_len // first_len)


def spectrum(columns):
    length, channels = columns.shape
    first_len, second_len = split_length(length)
    lower_half = first_len // 2
    whole_len = first_len * second_len
    values = columns.astype(jnp.float32).reshape(lower_half, second_len * channels)
    cos_first, sin_first = angle_tables(first_len, lower_half, first_len)
    real_one = jnp.dot(cos_first, values, precision=highest).reshape(
        first_len, second_len, channels
    )
    imag_one = -jnp.dot(sin_first, values, precision=highest).reshape(
        first_len, second_len, channels
    )
    twist_cos, twist_sin = angle_tables(first_len, second_len, whole_len)
    twist_cos = twist_cos[:, :, None]
    twist_sin = twist_sin[:, :, None]
    real_two = real_one * twist_cos + imag_one * twist_sin
    imag_two = imag_one * twist_cos - real_one * twist_sin
    cos_second, sin_second = angle_tables(second_len, second_len, second_len)
    real_out = jnp.einsum("amc,ml->alc", real_two, cos_second, precision=highest) + jnp.einsum(
        "amc,ml->alc", imag_two, sin_second, precision=highest
    )
    imag_out = jnp.einsum("amc,ml->alc", imag_two, cos_second, precision=highest) - jnp.einsum(
        "amc,ml->alc", real_two, sin_second, precision=highest
    )
    return (real_out, imag_out)


def signal(real_in, imag_in):
    first_len, second_len, channels = real_in.shape
    lower_half = first_len // 2
    whole_len = first_len * second_len
    cos_second, sin_second = angle_tables(second_len, second_len, second_len)
    real_one = jnp.einsum("alc,lm->amc", real_in, cos_second, precision=highest) - jnp.einsum(
        "alc,lm->amc", imag_in, sin_second, precision=highest
    )
    imag_one = jnp.einsum("alc,lm->amc", real_in, sin_second, precision=highest) + jnp.einsum(
        "alc,lm->amc", imag_in, cos_second, precision=highest
    )
    twist_cos, twist_sin = angle_tables(first_len, second_len, whole_len)
    twist_cos = twist_cos[:, :, None]
    twist_sin = twist_sin[:, :, None]
    real_two = real_one * twist_cos - imag_one * twist_sin
    imag_two = real_one * twist_sin + imag_one * twist_cos
    cos_first, sin_first = angle_tables(lower_half, first_len, first_len)
    merged = jnp.dot(
        cos_first, real_two.reshape(first_len, second_len * channels), precision=highest
    ) - jnp.dot(sin_first, imag_two.reshape(first_len, second_len * channels), precision=highest)
    return merged.reshape(lower_half * second_len, channels) / whole_len


def complex_product(left_real, left_imag, right_real, right_imag):
    return (
        left_real * right_real - left_imag * right_imag,
        left_real * right_imag + left_imag * right_real,
    )


def conj_product(left_real, left_imag, right_real, right_imag):
    return (
        left_real * right_real + left_imag * right_imag,
        left_imag * right_real - left_real * right_imag,
    )


def times_bf16(left_array, right_array):
    return (left_array.astype(jnp.float32) * right_array.astype(jnp.float32)).astype(jnp.bfloat16)


def output_grad(cotangent, out_weight, ready):
    weight_rows = lax.all_gather(out_weight, "lo", axis=0, tiled=True)
    token_rows = lax.all_gather(cotangent, "hi", axis=0, tiled=True)
    weight_rows, token_rows, _ = lax.optimization_barrier((weight_rows, token_rows, ready))
    partial_value = lax.dot_general(
        token_rows,
        weight_rows,
        (((1,), (1,)), ((), ())),
        preferred_element_type=jnp.float32,
    ).astype(jnp.bfloat16)
    tp_parts = lax.axis_size("tp")
    chunks = partial_value.reshape((tp_parts, -1) + partial_value.shape[1:])
    received = lax.all_to_all(chunks, "tp", split_axis=0, concat_axis=0, tiled=True)
    summed = jnp.sum(received.astype(jnp.float32), axis=0).astype(jnp.bfloat16)
    hi_count = lax.axis_size("hi")
    tp_count = lax.axis_size("tp")
    pairs = [
        (row * tp_count + col, col * tp_count + row)
        for row in range(hi_count)
        for col in range(tp_count)
    ]
    return lax.ppermute(summed, ("hi", "tp"), pairs)


Z_ORDER = (0, 1, 2, 3, 6, 7, 4, 5)


def butterfly_labels(devices):
    if devices != 4 * len(Z_ORDER):
        return list(range(devices))
    return [
        (index // 16) * 16 + Z_ORDER[(index // 2) % 8] * 2 + index % 2
        for index in range(devices)
    ]


def butterfly_sum(value, axis):
    devices = lax.axis_size(axis)
    labels = butterfly_labels(devices)
    owner = {label: index for index, label in enumerate(labels)}
    stride = 1
    while stride < devices:
        pairs = [(i, owner[labels[i] ^ stride]) for i in range(devices)]
        value = value + lax.ppermute(value, axis, pairs)
        stride *= 2
    return value


def body(proj, cotangent, out_weight, short_weight, long_filter):
    tok_rows = proj.shape[0]
    channels = proj.shape[2]
    taps_count = short_weight.shape[0]
    rim_rows = taps_count - 1
    lower_rows = shifted(proj[tok_rows - rim_rows :], SEQ, 1)
    extended = jnp.concatenate([lower_rows, proj], axis=0)
    primed = short_weight[0] * extended[rim_rows : rim_rows + tok_rows]
    for offset in range(1, taps_count):
        primed = (
            primed
            + short_weight[offset] * extended[rim_rows - offset : rim_rows - offset + tok_rows]
        )
    primed = primed.astype(jnp.bfloat16)
    query_conv = primed[:, 0]
    keys_conv = primed[:, 1]
    value_conv = primed[:, 2]
    gated_input = times_bf16(keys_conv, value_conv)
    filter_cols = lax.all_to_all(
        long_filter.astype(jnp.bfloat16), SEQ, split_axis=1, concat_axis=0, tiled=True
    ).astype(long_filter.dtype)
    filter_real, filter_imag = spectrum(filter_cols)
    gated_cols = lax.all_to_all(gated_input, SEQ, split_axis=1, concat_axis=0, tiled=True)
    gated_real, gated_imag = spectrum(gated_cols)
    conv_cols = signal(*complex_product(gated_real, gated_imag, filter_real, filter_imag)).astype(
        jnp.bfloat16
    )
    conv_out = lax.all_to_all(conv_cols, SEQ, split_axis=0, concat_axis=1, tiled=True)
    grad_out = output_grad(cotangent, out_weight, conv_out)
    grad_query = times_bf16(grad_out, conv_out)
    grad_conv = times_bf16(grad_out, query_conv)
    grad_cols = lax.all_to_all(grad_conv, SEQ, split_axis=1, concat_axis=0, tiled=True)
    grad_real, grad_imag = spectrum(grad_cols)
    gated_grad_cols = signal(*conj_product(grad_real, grad_imag, filter_real, filter_imag)).astype(
        jnp.bfloat16
    )
    filter_grad_cols = signal(*conj_product(grad_real, grad_imag, gated_real, gated_imag))
    gated_grad = lax.all_to_all(gated_grad_cols, SEQ, split_axis=0, concat_axis=1, tiled=True)
    grad_filter = lax.all_to_all(
        filter_grad_cols.astype(jnp.bfloat16), SEQ, split_axis=0, concat_axis=1, tiled=True
    ).astype(filter_grad_cols.dtype)
    grad_keys = times_bf16(gated_grad, value_conv)
    grad_value = times_bf16(gated_grad, keys_conv)
    grad_primed = jnp.stack([grad_query, grad_keys, grad_value], axis=1)
    next_rows = shifted(grad_primed[:rim_rows], SEQ, -1)
    trailing = jnp.concatenate([grad_primed, next_rows], axis=0)
    grad_sum = short_weight[0] * trailing[0:tok_rows]
    for offset in range(1, taps_count):
        grad_sum = grad_sum + short_weight[offset] * trailing[offset : offset + tok_rows]
    grad_proj = grad_sum.astype(jnp.bfloat16)
    grad_wide = grad_primed.astype(jnp.float32)
    local_short = jnp.stack(
        [
            jnp.sum(
                grad_wide
                * extended[rim_rows - offset : rim_rows - offset + tok_rows].astype(jnp.float32),
                axis=0,
            )
            for offset in range(taps_count)
        ]
    )
    grad_short = butterfly_sum(local_short, SEQ)
    return (grad_proj, grad_short, grad_filter)


def solution(mesh):
    seq_count = mesh.shape["seq"]
    tp_count = mesh.shape["tp"]
    split_mesh = jax.sharding.Mesh(
        mesh.devices.reshape(tp_count, seq_count // tp_count, tp_count), ("hi", "lo", "tp")
    )
    in_specs = (
        P(SEQ, None, "tp"),
        P(SEQ, "tp"),
        P(SEQ, "tp"),
        P(None, None, "tp"),
        P(SEQ, "tp"),
    )
    out_specs = (P(SEQ, None, "tp"), P(None, None, "tp"), P(SEQ, "tp"))
    return jax.shard_map(
        body, mesh=split_mesh, in_specs=in_specs, out_specs=out_specs, check_vma=False
    )
```
